512 devices in a mesh: dp: 64 (over z, x), tensor: 8 (over y, core).
Axes of the slice: x: 4, y: 4, z: 16, core: 2. Of those that a mesh axis runs over, the one named last changes fastest.
Arguments:
- queries: bfloat16 [8192, 8192], P('dp', 'tensor'), may hold values from -160 to 160, as said below
- key_cache_table: bfloat16 [8192, 32, 1024], P('dp', None, 'tensor'), may hold values from -4.5 to 4.5, as said below
- value_cache_table: bfloat16 [8192, 32, 1024], P('dp', None, 'tensor'), may hold values from -6 to 6
- filled_lengths: int32 [8192], P('dp'), may hold values from 8 to 32, as said below
- request_adapter: int32 [8192], replicated, may hold values from 0 to 1023, as said below
- adapter_store_row: int32 [1024], replicated, may hold values from 0 to 1023, as said below
- adapter_factor: float32 [1024], replicated, may hold values from 1 to 8
- adapter_down_store: bfloat16 [1024, 16, 8192], P('dp', None, 'tensor'), may hold values from -0.0625 to 0.0625
- adapter_up_store: bfloat16 [1024, 16, 8192], P('dp', None, 'tensor'), may hold values from -1.5 to 1.5
Outputs:
- attended: bfloat16 [8192, 8192], P('dp', 'tensor')
- adapter_delta: bfloat16 [8192, 8192], P('dp', 'tensor')
The draws below stay inside these ranges and needn't reach their ends.
Inputs may be any that keep to these rules, and one draw needn't show every extreme that they name: A custom draw; in the hidden draw some queries are aligned with keys of the same request. `key_cache_table`: A custom draw. `filled_lengths`: some request has all 32 slots filled. A permutation: adapter a is held by store shard adapter_store_row[a] // 16. `request_adapter`: in each aligned block of 128 requests (one group), at most 4 requests name adapters held by one store shard; every group reaches 4 for some shard, and one shard receives 4 from every group.
All inputs are finite; a program needn't handle non-finite values.
Results may differ from the reference program's by a relative error of at most 0.0064.
Values may be sent and summed in bfloat16 or wider, within the bound.
No kernel may reach another device: no remote copies, remote signals or barrier semaphores. Data moves between devices by JAX's collectives and lax.ppermute only.
A program may use at most 128 MiB of HBM per device.

```python
import math
import jax
import jax.numpy as jnp
from jax import lax

QUERY_HEADS = 64
KEY_VALUE_HEADS = 8
HEAD_WIDTH = 128
ADAPTER_RANK = 16
GROUP_REQUESTS = 128
CACHE_SLOTS = 32
ADP_DEV = 16
ADAPTER_TOTAL = 1024
REQUEST_TOTAL = 8192
N_DP = 64


def shared_place(key):
    return jax.random.permutation(jax.random.fold_in(key, 7), ADAPTER_TOTAL).astype(jnp.int32)


def leading_keys(key):
    return jnp.clip(jax.random.normal(jax.random.fold_in(key, 11), (REQUEST_TOTAL, 1, KEY_VALUE_HEADS * HEAD_WIDTH), jnp.float32), -4.5, 4.5)


def later_keys(key):
    return jnp.clip(jax.random.normal(jax.random.fold_in(key, 12), (REQUEST_TOTAL, CACHE_SLOTS - 1, KEY_VALUE_HEADS * HEAD_WIDTH), jnp.float32), -4.5, 4.5)


def draw_adapter_store_row(key, part):
    return shared_place(key)


def draw_request_adapter(key, part):
    place = shared_place(key)
    inverse = jnp.zeros((ADAPTER_TOTAL,), jnp.int32).at[place].set(jnp.arange(ADAPTER_TOTAL, dtype=jnp.int32))
    capacity = max(2, 2 * GROUP_REQUESTS // N_DP)
    base_key = jax.random.fold_in(key, 21)
    hot_shard = jax.random.randint(jax.random.fold_in(base_key, 1), (), 0, N_DP)

    def one_group(group_key):
        key_one, key_two, key_three, key_four = jax.random.split(group_key, 4)
        cells = jax.random.permutation(key_one, (N_DP - 1) * capacity)[:GROUP_REQUESTS - capacity].astype(jnp.int32)
        others = cells // capacity
        others = others + (others >= hot_shard).astype(jnp.int32)
        shards = jnp.concatenate([jnp.full((capacity,), hot_shard, jnp.int32), others])
        shards = shards[jax.random.permutation(key_two, GROUP_REQUESTS)]
        first_slot = jax.random.randint(key_three, (GROUP_REQUESTS,), 0, ADP_DEV)
        second_slot = jax.random.randint(key_four, (GROUP_REQUESTS,), 0, ADP_DEV)
        store_slot = jnp.minimum(first_slot, second_slot)
        return inverse[shards * ADP_DEV + store_slot]
    group_keys = jax.random.split(jax.random.fold_in(base_key, 2), N_DP)
    return jax.vmap(one_group)(group_keys).reshape(REQUEST_TOTAL).astype(jnp.int32)


def draw_filled_lengths(key, part):
    lowest = max(2, CACHE_SLOTS // 4)
    values = jax.random.randint(jax.random.fold_in(key, 31), (REQUEST_TOTAL,), lowest, CACHE_SLOTS + 1)
    chosen = jax.random.randint(jax.random.fold_in(key, 32), (), 0, REQUEST_TOTAL)
    return values.at[chosen].set(CACHE_SLOTS).astype(jnp.int32)


def draw_key_cache_table(key, part):
    first = leading_keys(key)
    later = later_keys(key)
    return jnp.concatenate([first, later], axis=1).astype(jnp.bfloat16)


def draw_queries(key, part):
    drawn = jax.random.normal(jax.random.fold_in(key, 13), (REQUEST_TOTAL, QUERY_HEADS * HEAD_WIDTH), jnp.float32)
    return jnp.clip(drawn, -6.0, 6.0).astype(jnp.bfloat16)


def block_scale(rng, dims, cuts, least, high):
    gain, own = 1.0, jax.random.fold_in(rng, 6)
    for axis_at, blocks in cuts:
        draws = jnp.exp(jax.random.uniform(jax.random.fold_in(own, axis_at), (blocks,), jnp.float32, least / len(cuts), high / len(cuts)))
        gain = gain * jnp.repeat(draws, dims[axis_at] // blocks).reshape([-1 if axis == axis_at else 1 for axis in range(len(dims))])
    return gain


def centred(stream_key, shape, spread, reach, cuts=(), kind=jnp.bfloat16):
    loudness = block_scale(stream_key, shape, cuts, -0.22, 0.18) if cuts else 1.0
    array = jax.random.normal(stream_key, shape, jnp.float32) * spread * loudness
    return jnp.minimum(jnp.maximum(array, -reach), reach).astype(kind)


def setup_inputs(seed: int = 0) -> dict:
    arg_keys = jax.random.split(jax.random.key(seed), 10)
    queries = draw_queries(jax.random.fold_in(arg_keys[9], 71), 0)
    key_cache_table = draw_key_cache_table(jax.random.fold_in(arg_keys[9], 71), 0)
    value_cache_table = centred(arg_keys[2], (REQUEST_TOTAL, CACHE_SLOTS, KEY_VALUE_HEADS * HEAD_WIDTH), 1.0, 6.0, ((0, 64), (2, 8)))
    filled_lengths = draw_filled_lengths(jax.random.fold_in(arg_keys[9], 71), 0)
    request_adapter = draw_request_adapter(jax.random.fold_in(arg_keys[9], 71), 0)
    adapter_store_row = draw_adapter_store_row(jax.random.fold_in(arg_keys[9], 71), 0)
    adapter_factor = jnp.clip(jnp.exp(jax.random.uniform(arg_keys[6], (ADAPTER_TOTAL,), jnp.float32, math.log(1.0), math.log(8.0))), 1.0, 8.0)
    adapter_down_store = centred(arg_keys[7], (ADAPTER_TOTAL, ADAPTER_RANK, QUERY_HEADS * HEAD_WIDTH), (QUERY_HEADS * HEAD_WIDTH) ** -0.5, 0.0625, ((0, 64), (2, 8)))
    adapter_up_store = centred(arg_keys[8], (ADAPTER_TOTAL, ADAPTER_RANK, QUERY_HEADS * HEAD_WIDTH), ADAPTER_RANK ** -0.5, 1.5, ((0, 64), (2, 8)))
    return {"queries": queries, "key_cache_table": key_cache_table, "value_cache_table": value_cache_table, "filled_lengths": filled_lengths, "request_adapter": request_adapter, "adapter_store_row": adapter_store_row, "adapter_factor": adapter_factor, "adapter_down_store": adapter_down_store, "adapter_up_store": adapter_up_store}


def reference(queries, key_cache_table, value_cache_table, filled_lengths, request_adapter, adapter_store_row, adapter_factor, adapter_down_store, adapter_up_store):
    group_width = QUERY_HEADS // KEY_VALUE_HEADS

    def one_group(block):
        rows_of_query, rows_of_key, rows_of_value, lengths, idents = block
        heads_of_query = rows_of_query.reshape(GROUP_REQUESTS, KEY_VALUE_HEADS, group_width, HEAD_WIDTH).astype(jnp.float32)
        heads_of_key = rows_of_key.reshape(GROUP_REQUESTS, CACHE_SLOTS, KEY_VALUE_HEADS, HEAD_WIDTH).astype(jnp.float32)
        heads_of_value = rows_of_value.reshape(GROUP_REQUESTS, CACHE_SLOTS, KEY_VALUE_HEADS, HEAD_WIDTH).astype(jnp.float32)
        scores = jnp.einsum('bkgd,blkd->bkgl', heads_of_query, heads_of_key) * (1.0 / math.sqrt(HEAD_WIDTH))
        visible = (jnp.arange(CACHE_SLOTS)[None, :] < lengths[:, None])[:, None, None, :]
        scores = jnp.where(visible, scores, jnp.float32(-1e+30))
        row_max = lax.optimization_barrier(jnp.max(scores, axis=-1, keepdims=True))
        exp_scores = jnp.exp(scores - row_max)
        weights = (exp_scores / lax.optimization_barrier(jnp.sum(exp_scores, axis=-1, keepdims=True))).astype(jnp.bfloat16)
        outputs = jnp.einsum('bkgl,blkd->bkgd', weights.astype(jnp.float32), heads_of_value)
        outputs = outputs.astype(jnp.bfloat16).reshape(GROUP_REQUESTS, QUERY_HEADS * HEAD_WIDTH)
        slot_position = adapter_store_row[idents]
        down_matrices = adapter_down_store[slot_position].astype(jnp.float32)
        up_matrices = adapter_up_store[slot_position].astype(jnp.float32)
        sums = jnp.einsum('bf,brf->br', outputs.astype(jnp.float32), down_matrices)
        low_rank = (sums * adapter_factor[idents][:, None]).astype(jnp.bfloat16)
        delta = jnp.einsum('br,brf->bf', low_rank.astype(jnp.float32), up_matrices).astype(jnp.bfloat16)
        return (outputs, delta)
    block_list = (queries.reshape(N_DP, GROUP_REQUESTS, QUERY_HEADS * HEAD_WIDTH), key_cache_table.reshape(N_DP, GROUP_REQUESTS, CACHE_SLOTS, KEY_VALUE_HEADS * HEAD_WIDTH), value_cache_table.reshape(N_DP, GROUP_REQUESTS, CACHE_SLOTS, KEY_VALUE_HEADS * HEAD_WIDTH), filled_lengths.reshape(N_DP, GROUP_REQUESTS), request_adapter.reshape(N_DP, GROUP_REQUESTS))
    outputs, delta = lax.map(one_group, block_list)
    return (outputs.reshape(REQUEST_TOTAL, QUERY_HEADS * HEAD_WIDTH), delta.reshape(REQUEST_TOTAL, QUERY_HEADS * HEAD_WIDTH))
```

```python
import math

import jax
import jax.numpy as jnp
from jax import lax
from jax.sharding import PartitionSpec as P

HEAD_WIDTH = 128


def of_everyone(value, axis):
    copies = jnp.broadcast_to(value, (lax.axis_size(axis), *value.shape))
    return lax.all_to_all(copies, axis, split_axis=0, concat_axis=0, tiled=True).sum(axis=0)


def attention(queries, key_cache_table, value_cache_table, filled_lengths):
    requests, row_width = queries.shape
    kv_local = key_cache_table.shape[2] // HEAD_WIDTH
    group_width = row_width // HEAD_WIDTH // kv_local
    length = key_cache_table.shape[1]
    heads_of_query = queries.reshape(requests, kv_local, group_width, HEAD_WIDTH)
    heads_of_key = key_cache_table.reshape(requests, length, kv_local, HEAD_WIDTH)
    heads_of_value = value_cache_table.reshape(requests, length, kv_local, HEAD_WIDTH)
    scores = jnp.einsum(
        "bkgd,blkd->bkgl", heads_of_query, heads_of_key, preferred_element_type=jnp.float32
    ) * (1.0 / math.sqrt(HEAD_WIDTH))
    visible = (jnp.arange(length)[None, :] < filled_lengths[:, None])[:, None, None, :]
    scores = jnp.where(visible, scores, jnp.float32(-1e30))
    row_max = jnp.max(scores, axis=-1, keepdims=True)
    exp_scores = jnp.exp(scores - row_max)
    weights = (exp_scores / jnp.sum(exp_scores, axis=-1, keepdims=True)).astype(jnp.bfloat16)
    attended = jnp.einsum(
        "bkgl,blkd->bkgd", weights, heads_of_value, preferred_element_type=jnp.float32
    )
    return attended.astype(jnp.bfloat16).reshape(requests, row_width)


def prefix_count(mask):
    n = mask.shape[-1]
    earlier = (jnp.arange(n)[:, None] < jnp.arange(n)[None, :]).astype(jnp.bfloat16)
    return jnp.einsum(
        "...i,ij->...j", mask.astype(jnp.bfloat16), earlier, preferred_element_type=jnp.float32
    )


def body(
    queries,
    key_cache_table,
    value_cache_table,
    filled_lengths,
    request_adapter,
    adapter_store_row,
    adapter_factor,
    adapter_down_store,
    adapter_up_store,
):
    requests, row_width = queries.shape
    group_count = lax.axis_size("dp")
    group_index = lax.axis_index("dp")
    capacity = max(2, 2 * requests // group_count)
    slot_count = group_count * capacity
    stored_total, rank_width = adapter_down_store.shape[0], adapter_down_store.shape[1]
    adapter_count = adapter_store_row.shape[0]

    attended = attention(queries, key_cache_table, value_cache_table, filled_lengths)

    own_ids = lax.dynamic_slice_in_dim(request_adapter, group_index * requests, requests)
    id_hot = own_ids[:, None] == jnp.arange(adapter_count)[None, :]
    own_row = jnp.sum(jnp.where(id_hot, adapter_store_row[None, :], 0), axis=1)
    own_dest = own_row // stored_total
    same_dest = own_dest[:, None] == own_dest[None, :]
    before = jnp.arange(requests)[:, None] > jnp.arange(requests)[None, :]
    own_order = jnp.sum((same_dest & before).astype(jnp.int32), axis=1)
    own_cell = own_dest * capacity + own_order
    cell_hot = own_cell[None, :] == jnp.arange(slot_count)[:, None]
    outgoing = jnp.einsum(
        "cb,bf->cf", cell_hot.astype(jnp.bfloat16), attended, preferred_element_type=jnp.float32
    ).astype(jnp.bfloat16)
    arrived = lax.all_to_all(
        outgoing.reshape(group_count, capacity, row_width), "dp", 0, 0, tiled=True
    ).reshape(slot_count, row_width)

    local_rows = group_index * stored_total + jnp.arange(stored_total)
    holds = adapter_store_row[None, :] == local_rows[:, None]
    local_ids = jnp.sum(jnp.where(holds, jnp.arange(adapter_count)[None, :], 0), axis=1)
    local_factor = jnp.sum(jnp.where(holds, adapter_factor[None, :], 0.0), axis=1)
    all_ids = request_adapter.reshape(group_count, requests)
    hit = (all_ids[:, :, None] == local_ids[None, None, :]).astype(jnp.bfloat16)
    mine = jnp.sum(hit, axis=2)
    order_in = prefix_count(mine)
    pick = (mine[:, None, :] > 0) & (
        order_in[:, None, :] == jnp.arange(capacity, dtype=jnp.float32)[None, :, None]
    )
    picked = jnp.einsum(
        "gcb,gbj->gcj", pick.astype(jnp.bfloat16), hit, preferred_element_type=jnp.float32
    ).reshape(slot_count, stored_total)
    item_scale = jnp.dot(picked, local_factor, precision=lax.Precision.HIGHEST)

    store_down = adapter_down_store.reshape(stored_total * rank_width, row_width)
    products = lax.dot_general(
        arrived, store_down, (((1,), (1,)), ((), ())), preferred_element_type=jnp.float32
    )
    partial_value = jnp.sum(
        products.reshape(slot_count, stored_total, rank_width) * picked[:, :, None], axis=1
    )
    summed = of_everyone(partial_value, "tensor")
    low_rank = (summed * item_scale[:, None]).astype(jnp.bfloat16)
    spread = (picked.astype(jnp.bfloat16)[:, :, None] * low_rank[:, None, :]).reshape(
        slot_count, stored_total * rank_width
    )
    store_up = adapter_up_store.reshape(stored_total * rank_width, row_width)
    result = jnp.dot(spread, store_up, preferred_element_type=jnp.float32).astype(jnp.bfloat16)
    returned = lax.all_to_all(
        result.reshape(group_count, capacity, row_width), "dp", 0, 0, tiled=True
    ).reshape(slot_count, row_width)
    adapter_delta = jnp.einsum(
        "cb,cf->bf", cell_hot.astype(jnp.bfloat16), returned, preferred_element_type=jnp.float32
    ).astype(jnp.bfloat16)
    return (attended, adapter_delta)


def solution(mesh):
    placed = (
        P("dp", "tensor"),
        P("dp", None, "tensor"),
        P("dp", None, "tensor"),
        P("dp"),
        P(),
        P(),
        P(),
        P("dp", None, "tensor"),
        P("dp", None, "tensor"),
    )
    return jax.shard_map(
        body,
        mesh=mesh,
        in_specs=placed,
        out_specs=(P("dp", "tensor"), P("dp", "tensor")),
        check_vma=False,
    )
```

```python
import math

import jax
import jax.numpy as jnp
from jax import lax
from jax.sharding import PartitionSpec as P

HEAD_WIDTH = 128


def of_everyone(value, axis):
    copies = jnp.broadcast_to(value, (lax.axis_size(axis), *value.shape))
    return lax.all_to_all(copies, axis, split_axis=0, concat_axis=0, tiled=True).sum(axis=0)


def attention(queries, key_cache_table, value_cache_table, filled_lengths):
    requests, row_width = queries.shape
    kv_local = key_cache_table.shape[2] // HEAD_WIDTH
    group_width = row_width // HEAD_WIDTH // kv_local
    length = key_cache_table.shape[1]
    heads_of_query = queries.reshape(requests, kv_local, group_width, HEAD_WIDTH)
    heads_of_key = key_cache_table.reshape(requests, length, kv_local, HEAD_WIDTH)
    heads_of_value = value_cache_table.reshape(requests, length, kv_local, HEAD_WIDTH)
    scores = jnp.einsum(
        "bkgd,blkd->bkgl", heads_of_query, heads_of_key, preferred_element_type=jnp.float32
    ) * (1.0 / math.sqrt(HEAD_WIDTH))
    visible = (jnp.arange(length)[None, :] < filled_lengths[:, None])[:, None, None, :]
    scores = jnp.where(visible, scores, jnp.float32(-1e30))
    row_max = jnp.max(scores, axis=-1, keepdims=True)
    exp_scores = jnp.exp(scores - row_max)
    weights = (exp_scores / jnp.sum(exp_scores, axis=-1, keepdims=True)).astype(jnp.bfloat16)
    attended = jnp.einsum(
        "bkgl,blkd->bkgd", weights, heads_of_value, preferred_element_type=jnp.float32
    )
    return attended.astype(jnp.bfloat16).reshape(requests, row_width)


def prefix_count(mask):
    n = mask.shape[-1]
    earlier = (jnp.arange(n)[:, None] < jnp.arange(n)[None, :]).astype(jnp.bfloat16)
    return jnp.einsum(
        "...i,ij->...j", mask.astype(jnp.bfloat16), earlier, preferred_element_type=jnp.float32
    )


def body(
    queries,
    key_cache_table,
    value_cache_table,
    filled_lengths,
    request_adapter,
    adapter_store_row,
    adapter_factor,
    adapter_down_store,
    adapter_up_store,
):
    requests, row_width = queries.shape
    group_count = lax.axis_size("dp")
    group_index = lax.axis_index("dp")
    capacity = max(2, 2 * requests // group_count)
    slot_count = group_count * capacity
    stored_total, rank_width = adapter_down_store.shape[0], adapter_down_store.shape[1]
    adapter_count = adapter_store_row.shape[0]

    attended = attention(queries, key_cache_table, value_cache_table, filled_lengths)

    all_ids = request_adapter.reshape(group_count, requests)
    own_group = jnp.arange(group_count)[:, None] == group_index
    own_ids = jnp.sum(jnp.where(own_group, all_ids, 0), axis=0)
    id_hot = own_ids[:, None] == jnp.arange(adapter_count)[None, :]
    own_row = jnp.sum(jnp.where(id_hot, adapter_store_row[None, :], 0), axis=1)
    own_dest = own_row // stored_total
    same_dest = own_dest[:, None] == own_dest[None, :]
    before = jnp.arange(requests)[:, None] > jnp.arange(requests)[None, :]
    own_order = jnp.sum((same_dest & before).astype(jnp.int32), axis=1)
    own_cell = own_dest * capacity + own_order
    cell_hot = (own_cell[None, :] == jnp.arange(slot_count)[:, None]).reshape(
        group_count, capacity, requests
    )
    outgoing = jnp.einsum(
        "dcb,bf->dcf", cell_hot.astype(jnp.bfloat16), attended, preferred_element_type=jnp.float32
    ).astype(jnp.bfloat16)
    arrived = lax.all_to_all(outgoing, "dp", 0, 0, tiled=True).reshape(slot_count, row_width)

    local_rows = group_index * stored_total + jnp.arange(stored_total)
    holds = adapter_store_row[None, :] == local_rows[:, None]
    local_ids = jnp.sum(jnp.where(holds, jnp.arange(adapter_count)[None, :], 0), axis=1)
    local_factor = jnp.sum(jnp.where(holds, adapter_factor[None, :], 0.0), axis=1)
    hit = (all_ids[:, :, None] == local_ids[None, None, :]).astype(jnp.bfloat16)
    mine = jnp.sum(hit, axis=2)
    order_in = prefix_count(mine)
    pick = (mine[:, None, :] > 0) & (
        order_in[:, None, :] == jnp.arange(capacity, dtype=jnp.float32)[None, :, None]
    )
    picked = jnp.einsum(
        "gcb,gbj->gcj", pick.astype(jnp.bfloat16), hit, preferred_element_type=jnp.float32
    ).reshape(slot_count, stored_total)
    item_scale = jnp.dot(picked, local_factor, precision=lax.Precision.HIGHEST)

    store_down = adapter_down_store.reshape(stored_total * rank_width, row_width)
    products = lax.dot_general(
        arrived, store_down, (((1,), (1,)), ((), ())), preferred_element_type=jnp.float32
    )
    partial_value = jnp.sum(
        products.reshape(slot_count, stored_total, rank_width) * picked[:, :, None], axis=1
    )
    summed = of_everyone(partial_value, "tensor")
    low_rank = (summed * item_scale[:, None]).astype(jnp.bfloat16)
    spread = (picked.astype(jnp.bfloat16)[:, :, None] * low_rank[:, None, :]).reshape(
        slot_count, stored_total * rank_width
    )
    store_up = adapter_up_store.reshape(stored_total * rank_width, row_width)
    result = jnp.dot(spread, store_up, preferred_element_type=jnp.float32).astype(jnp.bfloat16)
    returned = lax.all_to_all(
        result.reshape(group_count, capacity, row_width), "dp", 0, 0, tiled=True
    ).reshape(slot_count, row_width)
    adapter_delta = jnp.take(returned, own_cell, axis=0)
    return (attended, adapter_delta)


def solution(mesh):
    placed = (
        P("dp", "tensor"),
        P("dp", None, "tensor"),
        P("dp", None, "tensor"),
        P("dp"),
        P(),
        P(),
        P(),
        P("dp", None, "tensor"),
        P("dp", None, "tensor"),
    )
    return jax.shard_map(
        body,
        mesh=mesh,
        in_specs=placed,
        out_specs=(P("dp", "tensor"), P("dp", "tensor")),
        check_vma=False,
    )
```

```python
import math

import jax
import jax.numpy as jnp
from jax import lax
from jax.experimental import pallas as pl
from jax.sharding import PartitionSpec as P

HEAD_WIDTH = 128
BLOCK_REQUESTS = 32


def of_everyone(value, axis):
    copies = jnp.broadcast_to(value, (lax.axis_size(axis), *value.shape))
    return lax.all_to_all(copies, axis, split_axis=0, concat_axis=0, tiled=True).sum(axis=0)


def attention(queries, key_cache_table, value_cache_table, filled_lengths):
    requests, row_width = queries.shape
    kv_local = key_cache_table.shape[2] // HEAD_WIDTH
    group_width = row_width // HEAD_WIDTH // kv_local
    length = key_cache_table.shape[1]
    heads_of_query = queries.reshape(requests, kv_local, group_width, HEAD_WIDTH)
    heads_of_key = key_cache_table.reshape(requests, length, kv_local, HEAD_WIDTH)
    heads_of_value = value_cache_table.reshape(requests, length, kv_local, HEAD_WIDTH)
    scores = jnp.einsum(
        "bkgd,blkd->bkgl", heads_of_query, heads_of_key, preferred_element_type=jnp.float32
    ) * (1.0 / math.sqrt(HEAD_WIDTH))
    visible = (jnp.arange(length)[None, :] < filled_lengths[:, None])[:, None, None, :]
    scores = jnp.where(visible, scores, jnp.float32(-1e30))
    row_max = jnp.max(scores, axis=-1, keepdims=True)
    exp_scores = jnp.exp(scores - row_max)
    weights = (exp_scores / jnp.sum(exp_scores, axis=-1, keepdims=True)).astype(jnp.bfloat16)
    attended = jnp.einsum(
        "bkgl,blkd->bkgd", weights, heads_of_value, preferred_element_type=jnp.float32
    )
    return attended.astype(jnp.bfloat16).reshape(requests, row_width)


def attention_kernel(q_ref, k_ref, v_ref, len_ref, out_ref):
    block = q_ref.shape[0]
    heads = q_ref.shape[1] // HEAD_WIDTH
    length = k_ref.shape[1]
    width = block * length
    q = q_ref[...]
    stacked = jnp.concatenate(
        [q[:, h * HEAD_WIDTH : (h + 1) * HEAD_WIDTH] for h in range(heads)], axis=0
    )
    keys = k_ref[...].reshape(width, HEAD_WIDTH)
    values = v_ref[...].reshape(width, HEAD_WIDTH)
    scores = lax.dot_general(
        stacked, keys, (((1,), (1,)), ((), ())), preferred_element_type=jnp.float32
    ) * (1.0 / math.sqrt(HEAD_WIDTH))
    lens = jnp.concatenate([len_ref[...]] * heads, axis=0)
    row_request = lax.broadcasted_iota(jnp.int32, (heads * block, width), 0) % block
    col = lax.broadcasted_iota(jnp.int32, (heads * block, width), 1)
    visible = (col // length == row_request) & (col % length < lens)
    scores = jnp.where(visible, scores, jnp.float32(-1e30))
    row_max = jnp.max(scores, axis=-1, keepdims=True)
    exp_scores = jnp.exp(scores - row_max)
    weights = (exp_scores / jnp.sum(exp_scores, axis=-1, keepdims=True)).astype(jnp.bfloat16)
    attended = jnp.dot(weights, values, preferred_element_type=jnp.float32).astype(jnp.bfloat16)
    for h in range(heads):
        out_ref[:, h * HEAD_WIDTH : (h + 1) * HEAD_WIDTH] = attended[h * block : (h + 1) * block]


def attention_pallas(queries, key_cache_table, value_cache_table, filled_lengths):
    requests, row_width = queries.shape
    length = key_cache_table.shape[1]
    kv_width = key_cache_table.shape[2]
    block = min(BLOCK_REQUESTS, requests)
    return pl.pallas_call(
        attention_kernel,
        grid=(requests // block,),
        in_specs=[
            pl.BlockSpec((block, row_width), lambda i: (i, 0)),
            pl.BlockSpec((block, length, kv_width), lambda i: (i, 0, 0)),
            pl.BlockSpec((block, length, kv_width), lambda i: (i, 0, 0)),
            pl.BlockSpec((block, 1), lambda i: (i, 0)),
        ],
        out_specs=pl.BlockSpec((block, row_width), lambda i: (i, 0)),
        out_shape=jax.ShapeDtypeStruct((requests, row_width), jnp.bfloat16),
    )(queries, key_cache_table, value_cache_table, filled_lengths.reshape(requests, 1))


def prefix_count(mask):
    n = mask.shape[-1]
    earlier = (jnp.arange(n)[:, None] < jnp.arange(n)[None, :]).astype(jnp.bfloat16)
    return jnp.einsum(
        "...i,ij->...j", mask.astype(jnp.bfloat16), earlier, preferred_element_type=jnp.float32
    )


def body(
    queries,
    key_cache_table,
    value_cache_table,
    filled_lengths,
    request_adapter,
    adapter_store_row,
    adapter_factor,
    adapter_down_store,
    adapter_up_store,
):
    requests, row_width = queries.shape
    group_count = lax.axis_size("dp")
    group_index = lax.axis_index("dp")
    capacity = max(2, 2 * requests // group_count)
    slot_count = group_count * capacity
    stored_total, rank_width = adapter_down_store.shape[0], adapter_down_store.shape[1]
    adapter_count = adapter_store_row.shape[0]

    if key_cache_table.shape[2] == HEAD_WIDTH:
        attended = attention_pallas(queries, key_cache_table, value_cache_table, filled_lengths)
    else:
        attended = attention(queries, key_cache_table, value_cache_table, filled_lengths)

    own_ids = lax.dynamic_slice_in_dim(request_adapter, group_index * requests, requests)
    id_hot = own_ids[:, None] == jnp.arange(adapter_count)[None, :]
    own_row = jnp.sum(jnp.where(id_hot, adapter_store_row[None, :], 0), axis=1)
    own_dest = own_row // stored_total
    same_dest = own_dest[:, None] == own_dest[None, :]
    before = jnp.arange(requests)[:, None] > jnp.arange(requests)[None, :]
    own_order = jnp.sum((same_dest & before).astype(jnp.int32), axis=1)
    own_cell = own_dest * capacity + own_order
    cell_hot = own_cell[None, :] == jnp.arange(slot_count)[:, None]
    outgoing = jnp.einsum(
        "cb,bf->cf", cell_hot.astype(jnp.bfloat16), attended, preferred_element_type=jnp.float32
    ).astype(jnp.bfloat16)
    arrived = lax.all_to_all(
        outgoing.reshape(group_count, capacity, row_width), "dp", 0, 0, tiled=True
    ).reshape(slot_count, row_width)

    local_rows = group_index * stored_total + jnp.arange(stored_total)
    holds = adapter_store_row[None, :] == local_rows[:, None]
    local_ids = jnp.sum(jnp.where(holds, jnp.arange(adapter_count)[None, :], 0), axis=1)
    local_factor = jnp.sum(jnp.where(holds, adapter_factor[None, :], 0.0), axis=1)
    all_ids = request_adapter.reshape(group_count, requests)
    hit = (all_ids[:, :, None] == local_ids[None, None, :]).astype(jnp.bfloat16)
    mine = jnp.sum(hit, axis=2)
    order_in = prefix_count(mine)
    pick = (mine[:, None, :] > 0) & (
        order_in[:, None, :] == jnp.arange(capacity, dtype=jnp.float32)[None, :, None]
    )
    picked = jnp.einsum(
        "gcb,gbj->gcj", pick.astype(jnp.bfloat16), hit, preferred_element_type=jnp.float32
    ).reshape(slot_count, stored_total)
    item_scale = jnp.dot(picked, local_factor, precision=lax.Precision.HIGHEST)

    store_down = adapter_down_store.reshape(stored_total * rank_width, row_width)
    products = lax.dot_general(
        arrived, store_down, (((1,), (1,)), ((), ())), preferred_element_type=jnp.float32
    )
    partial_value = jnp.sum(
        products.reshape(slot_count, stored_total, rank_width) * picked[:, :, None], axis=1
    )
    summed = of_everyone(partial_value, "tensor")
    low_rank = (summed * item_scale[:, None]).astype(jnp.bfloat16)
    spread = (picked.astype(jnp.bfloat16)[:, :, None] * low_rank[:, None, :]).reshape(
        slot_count, stored_total * rank_width
    )
    store_up = adapter_up_store.reshape(stored_total * rank_width, row_width)
    result = jnp.dot(spread, store_up, preferred_element_type=jnp.float32).astype(jnp.bfloat16)
    returned = lax.all_to_all(
        result.reshape(group_count, capacity, row_width), "dp", 0, 0, tiled=True
    ).reshape(slot_count, row_width)
    adapter_delta = jnp.einsum(
        "cb,cf->bf", cell_hot.astype(jnp.bfloat16), returned, preferred_element_type=jnp.float32
    ).astype(jnp.bfloat16)
    return (attended, adapter_delta)


def solution(mesh):
    placed = (
        P("dp", "tensor"),
        P("dp", None, "tensor"),
        P("dp", None, "tensor"),
        P("dp"),
        P(),
        P(),
        P(),
        P("dp", None, "tensor"),
        P("dp", None, "tensor"),
    )
    return jax.shard_map(
        body,
        mesh=mesh,
        in_specs=placed,
        out_specs=(P("dp", "tensor"), P("dp", "tensor")),
        check_vma=False,
    )
```

```python
import math

import jax
import jax.numpy as jnp
from jax import lax
from jax.experimental import pallas as pl
from jax.sharding import PartitionSpec as P

HEAD_WIDTH = 128


def of_everyone(value, axis):
    copies = jnp.broadcast_to(value, (lax.axis_size(axis), *value.shape))
    return lax.all_to_all(copies, axis, split_axis=0, concat_axis=0, tiled=True).sum(axis=0)


def attention(queries, key_cache_table, value_cache_table, filled_lengths):
    requests, row_width = queries.shape
    kv_local = key_cache_table.shape[2] // HEAD_WIDTH
    group_width = row_width // HEAD_WIDTH // kv_local
    length = key_cache_table.shape[1]
    heads_of_query = queries.reshape(requests, kv_local, group_width, HEAD_WIDTH)
    heads_of_key = key_cache_table.reshape(requests, length, kv_local, HEAD_WIDTH)
    heads_of_value = value_cache_table.reshape(requests, length, kv_local, HEAD_WIDTH)
    scores = jnp.einsum(
        "bkgd,blkd->bkgl", heads_of_query, heads_of_key, preferred_element_type=jnp.float32
    ) * (1.0 / math.sqrt(HEAD_WIDTH))
    visible = (jnp.arange(length)[None, :] < filled_lengths[:, None])[:, None, None, :]
    scores = jnp.where(visible, scores, jnp.float32(-1e30))
    row_max = jnp.max(scores, axis=-1, keepdims=True)
    exp_scores = jnp.exp(scores - row_max)
    weights = (exp_scores / jnp.sum(exp_scores, axis=-1, keepdims=True)).astype(jnp.bfloat16)
    attended = jnp.einsum(
        "bkgl,blkd->bkgd", weights, heads_of_value, preferred_element_type=jnp.float32
    )
    return attended.astype(jnp.bfloat16).reshape(requests, row_width)


def pack_kernel(hot_ref, rows_ref, out_ref):
    capacity = out_ref.shape[1]
    full = jnp.dot(hot_ref[...], rows_ref[...], preferred_element_type=jnp.float32)
    for d in range(out_ref.shape[0]):
        out_ref[d] = full[d * capacity : (d + 1) * capacity].astype(out_ref.dtype)


def pack_rows(hot, rows, group_count, capacity):
    return pl.pallas_call(
        pack_kernel,
        out_shape=jax.ShapeDtypeStruct((group_count, capacity, rows.shape[1]), rows.dtype),
    )(hot, rows)


def prefix_count(mask):
    n = mask.shape[-1]
    earlier = (jnp.arange(n)[:, None] < jnp.arange(n)[None, :]).astype(jnp.bfloat16)
    return jnp.einsum(
        "...i,ij->...j", mask.astype(jnp.bfloat16), earlier, preferred_element_type=jnp.float32
    )


def body(
    queries,
    key_cache_table,
    value_cache_table,
    filled_lengths,
    request_adapter,
    adapter_store_row,
    adapter_factor,
    adapter_down_store,
    adapter_up_store,
):
    requests, row_width = queries.shape
    group_count = lax.axis_size("dp")
    group_index = lax.axis_index("dp")
    capacity = max(2, 2 * requests // group_count)
    slot_count = group_count * capacity
    stored_total, rank_width = adapter_down_store.shape[0], adapter_down_store.shape[1]
    adapter_count = adapter_store_row.shape[0]

    attended = attention(queries, key_cache_table, value_cache_table, filled_lengths)

    own_ids = lax.dynamic_slice_in_dim(request_adapter, group_index * requests, requests)
    id_hot = own_ids[:, None] == jnp.arange(adapter_count)[None, :]
    own_row = jnp.sum(jnp.where(id_hot, adapter_store_row[None, :], 0), axis=1)
    own_dest = own_row // stored_total
    same_dest = own_dest[:, None] == own_dest[None, :]
    before = jnp.arange(requests)[:, None] > jnp.arange(requests)[None, :]
    own_order = jnp.sum((same_dest & before).astype(jnp.int32), axis=1)
    own_cell = own_dest * capacity + own_order
    cell_hot = own_cell[None, :] == jnp.arange(slot_count)[:, None]
    outgoing = pack_rows(cell_hot.astype(jnp.bfloat16), attended, group_count, capacity)
    arrived = lax.all_to_all(outgoing, "dp", 0, 0, tiled=True).reshape(slot_count, row_width)

    local_rows = group_index * stored_total + jnp.arange(stored_total)
    holds = adapter_store_row[None, :] == local_rows[:, None]
    local_ids = jnp.sum(jnp.where(holds, jnp.arange(adapter_count)[None, :], 0), axis=1)
    local_factor = jnp.sum(jnp.where(holds, adapter_factor[None, :], 0.0), axis=1)
    all_ids = request_adapter.reshape(group_count, requests)
    hit = (all_ids[:, :, None] == local_ids[None, None, :]).astype(jnp.bfloat16)
    mine = jnp.sum(hit, axis=2)
    order_in = prefix_count(mine)
    pick = (mine[:, None, :] > 0) & (
        order_in[:, None, :] == jnp.arange(capacity, dtype=jnp.float32)[None, :, None]
    )
    picked = jnp.einsum(
        "gcb,gbj->gcj", pick.astype(jnp.bfloat16), hit, preferred_element_type=jnp.float32
    ).reshape(slot_count, stored_total)
    item_scale = jnp.dot(picked, local_factor, precision=lax.Precision.HIGHEST)

    store_down = adapter_down_store.reshape(stored_total * rank_width, row_width)
    products = lax.dot_general(
        arrived, store_down, (((1,), (1,)), ((), ())), preferred_element_type=jnp.float32
    )
    partial_value = jnp.sum(
        products.reshape(slot_count, stored_total, rank_width) * picked[:, :, None], axis=1
    )
    summed = of_everyone(partial_value, "tensor")
    low_rank = (summed * item_scale[:, None]).astype(jnp.bfloat16)
    spread = (picked.astype(jnp.bfloat16)[:, :, None] * low_rank[:, None, :]).reshape(
        slot_count, stored_total * rank_width
    )
    store_up = adapter_up_store.reshape(stored_total * rank_width, row_width)
    result = jnp.dot(spread, store_up, preferred_element_type=jnp.float32).astype(jnp.bfloat16)
    returned = lax.all_to_all(
        result.reshape(group_count, capacity, row_width), "dp", 0, 0, tiled=True
    ).reshape(slot_count, row_width)
    adapter_delta = jnp.einsum(
        "cb,cf->bf", cell_hot.astype(jnp.bfloat16), returned, preferred_element_type=jnp.float32
    ).astype(jnp.bfloat16)
    return (attended, adapter_delta)


def solution(mesh):
    placed = (
        P("dp", "tensor"),
        P("dp", None, "tensor"),
        P("dp", None, "tensor"),
        P("dp"),
        P(),
        P(),
        P(),
        P("dp", None, "tensor"),
        P("dp", None, "tensor"),
    )
    return jax.shard_map(
        body,
        mesh=mesh,
        in_specs=placed,
        out_specs=(P("dp", "tensor"), P("dp", "tensor")),
        check_vma=False,
    )
```

```python
import math

import jax
import jax.numpy as jnp
from jax import lax
from jax.sharding import PartitionSpec as P

HEAD_WIDTH = 128
BLOCK_REQUESTS = 4


def of_everyone(value, axis):
    copies = jnp.broadcast_to(value, (lax.axis_size(axis), *value.shape))
    return lax.all_to_all(copies, axis, split_axis=0, concat_axis=0, tiled=True).sum(axis=0)


def attention(queries, key_cache_table, value_cache_table, filled_lengths):
    requests, row_width = queries.shape
    kv_local = key_cache_table.shape[2] // HEAD_WIDTH
    group_width = row_width // HEAD_WIDTH // kv_local
    length = key_cache_table.shape[1]
    heads_of_query = queries.reshape(requests, kv_local, group_width, HEAD_WIDTH)
    heads_of_key = key_cache_table.reshape(requests, length, kv_local, HEAD_WIDTH)
    heads_of_value = value_cache_table.reshape(requests, length, kv_local, HEAD_WIDTH)
    scores = jnp.einsum(
        "bkgd,blkd->bkgl", heads_of_query, heads_of_key, preferred_element_type=jnp.float32
    ) * (1.0 / math.sqrt(HEAD_WIDTH))
    visible = (jnp.arange(length)[None, :] < filled_lengths[:, None])[:, None, None, :]
    scores = jnp.where(visible, scores, jnp.float32(-1e30))
    row_max = jnp.max(scores, axis=-1, keepdims=True)
    exp_scores = jnp.exp(scores - row_max)
    weights = (exp_scores / jnp.sum(exp_scores, axis=-1, keepdims=True)).astype(jnp.bfloat16)
    attended = jnp.einsum(
        "bkgl,blkd->bkgd", weights, heads_of_value, preferred_element_type=jnp.float32
    )
    return attended.astype(jnp.bfloat16).reshape(requests, row_width)


def attention_blocked(queries, key_cache_table, value_cache_table, filled_lengths):
    requests, row_width = queries.shape
    heads = row_width // HEAD_WIDTH
    length = key_cache_table.shape[1]
    block = BLOCK_REQUESTS
    count = requests // block
    stacked = (
        queries.reshape(count, block, heads, HEAD_WIDTH)
        .transpose(0, 2, 1, 3)
        .reshape(count, heads * block, HEAD_WIDTH)
    )
    keys = key_cache_table.reshape(count, block * length, HEAD_WIDTH)
    values = value_cache_table.reshape(count, block * length, HEAD_WIDTH)
    scores = jnp.einsum(
        "nrd,njd->nrj", stacked, keys, preferred_element_type=jnp.float32
    ) * (1.0 / math.sqrt(HEAD_WIDTH))
    row_request = jnp.arange(heads * block) % block
    col_request = jnp.arange(block * length) // length
    col_slot = jnp.arange(block * length) % length
    col_length = jnp.repeat(filled_lengths.reshape(count, block), length, axis=1)
    visible = (row_request[:, None] == col_request[None, :])[None] & (
        col_slot[None, None, :] < col_length[:, None, :]
    )
    scores = jnp.where(visible, scores, jnp.float32(-1e30))
    row_max = jnp.max(scores, axis=-1, keepdims=True)
    exp_scores = jnp.exp(scores - row_max)
    weights = (exp_scores / jnp.sum(exp_scores, axis=-1, keepdims=True)).astype(jnp.bfloat16)
    attended = jnp.einsum("nrj,njd->nrd", weights, values, preferred_element_type=jnp.float32)
    return (
        attended.astype(jnp.bfloat16)
        .reshape(count, heads, block, HEAD_WIDTH)
        .transpose(0, 2, 1, 3)
        .reshape(requests, row_width)
    )


def prefix_count(mask):
    n = mask.shape[-1]
    earlier = (jnp.arange(n)[:, None] < jnp.arange(n)[None, :]).astype(jnp.bfloat16)
    return jnp.einsum(
        "...i,ij->...j", mask.astype(jnp.bfloat16), earlier, preferred_element_type=jnp.float32
    )


def body(
    queries,
    key_cache_table,
    value_cache_table,
    filled_lengths,
    request_adapter,
    adapter_store_row,
    adapter_factor,
    adapter_down_store,
    adapter_up_store,
):
    requests, row_width = queries.shape
    group_count = lax.axis_size("dp")
    group_index = lax.axis_index("dp")
    capacity = max(2, 2 * requests // group_count)
    slot_count = group_count * capacity
    stored_total, rank_width = adapter_down_store.shape[0], adapter_down_store.shape[1]
    adapter_count = adapter_store_row.shape[0]

    if key_cache_table.shape[2] == HEAD_WIDTH and requests % BLOCK_REQUESTS == 0:
        attended = attention_blocked(queries, key_cache_table, value_cache_table, filled_lengths)
    else:
        attended = attention(queries, key_cache_table, value_cache_table, filled_lengths)

    own_ids = lax.dynamic_slice_in_dim(request_adapter, group_index * requests, requests)
    id_hot = own_ids[:, None] == jnp.arange(adapter_count)[None, :]
    own_row = jnp.sum(jnp.where(id_hot, adapter_store_row[None, :], 0), axis=1)
    own_dest = own_row // stored_total
    same_dest = own_dest[:, None] == own_dest[None, :]
    before = jnp.arange(requests)[:, None] > jnp.arange(requests)[None, :]
    own_order = jnp.sum((same_dest & before).astype(jnp.int32), axis=1)
    own_cell = own_dest * capacity + own_order
    cell_hot = own_cell[None, :] == jnp.arange(slot_count)[:, None]
    outgoing = jnp.einsum(
        "cb,bf->cf", cell_hot.astype(jnp.bfloat16), attended, preferred_element_type=jnp.float32
    ).astype(jnp.bfloat16)
    arrived = lax.all_to_all(
        outgoing.reshape(group_count, capacity, row_width), "dp", 0, 0, tiled=True
    ).reshape(slot_count, row_width)

    local_rows = group_index * stored_total + jnp.arange(stored_total)
    holds = adapter_store_row[None, :] == local_rows[:, None]
    local_ids = jnp.sum(jnp.where(holds, jnp.arange(adapter_count)[None, :], 0), axis=1)
    local_factor = jnp.sum(jnp.where(holds, adapter_factor[None, :], 0.0), axis=1)
    all_ids = request_adapter.reshape(group_count, requests)
    hit = (all_ids[:, :, None] == local_ids[None, None, :]).astype(jnp.bfloat16)
    mine = jnp.sum(hit, axis=2)
    order_in = prefix_count(mine)
    pick = (mine[:, None, :] > 0) & (
        order_in[:, None, :] == jnp.arange(capacity, dtype=jnp.float32)[None, :, None]
    )
    picked = jnp.einsum(
        "gcb,gbj->gcj", pick.astype(jnp.bfloat16), hit, preferred_element_type=jnp.float32
    ).reshape(slot_count, stored_total)
    item_scale = jnp.dot(picked, local_factor, precision=lax.Precision.HIGHEST)

    store_down = adapter_down_store.reshape(stored_total * rank_width, row_width)
    products = lax.dot_general(
        arrived, store_down, (((1,), (1,)), ((), ())), preferred_element_type=jnp.float32
    )
    partial_value = jnp.sum(
        products.reshape(slot_count, stored_total, rank_width) * picked[:, :, None], axis=1
    )
    summed = of_everyone(partial_value, "tensor")
    low_rank = (summed * item_scale[:, None]).astype(jnp.bfloat16)
    spread = (picked.astype(jnp.bfloat16)[:, :, None] * low_rank[:, None, :]).reshape(
        slot_count, stored_total * rank_width
    )
    store_up = adapter_up_store.reshape(stored_total * rank_width, row_width)
    result = jnp.dot(spread, store_up, preferred_element_type=jnp.float32).astype(jnp.bfloat16)
    returned = lax.all_to_all(
        result.reshape(group_count, capacity, row_width), "dp", 0, 0, tiled=True
    ).reshape(slot_count, row_width)
    adapter_delta = jnp.einsum(
        "cb,cf->bf", cell_hot.astype(jnp.bfloat16), returned, preferred_element_type=jnp.float32
    ).astype(jnp.bfloat16)
    return (attended, adapter_delta)


def solution(mesh):
    placed = (
        P("dp", "tensor"),
        P("dp", None, "tensor"),
        P("dp", None, "tensor"),
        P("dp"),
        P(),
        P(),
        P(),
        P("dp", None, "tensor"),
        P("dp", None, "tensor"),
    )
    return jax.shard_map(
        body,
        mesh=mesh,
        in_specs=placed,
        out_specs=(P("dp", "tensor"), P("dp", "tensor")),
        check_vma=False,
    )
```

```python
import math

import jax
import jax.numpy as jnp
from jax import lax
from jax.sharding import PartitionSpec as P

HEAD_WIDTH = 128
BLOCK_REQUESTS = 4


def of_everyone(value, axis):
    copies = jnp.broadcast_to(value, (lax.axis_size(axis), *value.shape))
    return lax.all_to_all(copies, axis, split_axis=0, concat_axis=0, tiled=True).sum(axis=0)


def attention(queries, key_cache_table, value_cache_table, filled_lengths):
    requests, row_width = queries.shape
    kv_local = key_cache_table.shape[2] // HEAD_WIDTH
    group_width = row_width // HEAD_WIDTH // kv_local
    length = key_cache_table.shape[1]
    heads_of_query = queries.reshape(requests, kv_local, group_width, HEAD_WIDTH)
    heads_of_key = key_cache_table.reshape(requests, length, kv_local, HEAD_WIDTH)
    heads_of_value = value_cache_table.reshape(requests, length, kv_local, HEAD_WIDTH)
    scores = jnp.einsum(
        "bkgd,blkd->bkgl", heads_of_query, heads_of_key, preferred_element_type=jnp.float32
    ) * (1.0 / math.sqrt(HEAD_WIDTH))
    visible = (jnp.arange(length)[None, :] < filled_lengths[:, None])[:, None, None, :]
    scores = jnp.where(visible, scores, jnp.float32(-1e30))
    row_max = jnp.max(scores, axis=-1, keepdims=True)
    exp_scores = jnp.exp(scores - row_max)
    weights = (exp_scores / jnp.sum(exp_scores, axis=-1, keepdims=True)).astype(jnp.bfloat16)
    attended = jnp.einsum(
        "bkgl,blkd->bkgd", weights, heads_of_value, preferred_element_type=jnp.float32
    )
    return attended.astype(jnp.bfloat16).reshape(requests, row_width)


def attention_blocked(queries, key_cache_table, value_cache_table, filled_lengths):
    requests, row_width = queries.shape
    heads = row_width // HEAD_WIDTH
    length = key_cache_table.shape[1]
    block = BLOCK_REQUESTS
    count = requests // block
    stacked = (
        queries.reshape(count, block, heads, HEAD_WIDTH)
        .transpose(0, 2, 1, 3)
        .reshape(count, heads * block, HEAD_WIDTH)
    )
    keys = key_cache_table.reshape(count, block * length, HEAD_WIDTH)
    values = value_cache_table.reshape(count, block * length, HEAD_WIDTH)
    scores = jnp.einsum(
        "nrd,njd->nrj", stacked, keys, preferred_element_type=jnp.float32
    ) * (1.0 / math.sqrt(HEAD_WIDTH))
    row_request = jnp.arange(heads * block) % block
    col_request = jnp.arange(block * length) // length
    col_slot = jnp.arange(block * length) % length
    col_length = jnp.repeat(filled_lengths.reshape(count, block), length, axis=1)
    visible = (row_request[:, None] == col_request[None, :])[None] & (
        col_slot[None, None, :] < col_length[:, None, :]
    )
    scores = jnp.where(visible, scores, jnp.float32(-1e30))
    row_max = jnp.max(scores, axis=-1, keepdims=True)
    exp_scores = jnp.exp(scores - row_max)
    weights = (exp_scores / jnp.sum(exp_scores, axis=-1, keepdims=True)).astype(jnp.bfloat16)
    weights = lax.optimization_barrier(weights)
    attended = jnp.einsum("nrj,njd->nrd", weights, values, preferred_element_type=jnp.float32)
    return (
        attended.astype(jnp.bfloat16)
        .reshape(count, heads, block, HEAD_WIDTH)
        .transpose(0, 2, 1, 3)
        .reshape(requests, row_width)
    )


def prefix_count(mask):
    n = mask.shape[-1]
    earlier = (jnp.arange(n)[:, None] < jnp.arange(n)[None, :]).astype(jnp.bfloat16)
    return jnp.einsum(
        "...i,ij->...j", mask.astype(jnp.bfloat16), earlier, preferred_element_type=jnp.float32
    )


def body(
    queries,
    key_cache_table,
    value_cache_table,
    filled_lengths,
    request_adapter,
    adapter_store_row,
    adapter_factor,
    adapter_down_store,
    adapter_up_store,
):
    requests, row_width = queries.shape
    group_count = lax.axis_size("dp")
    group_index = lax.axis_index("dp")
    capacity = max(2, 2 * requests // group_count)
    slot_count = group_count * capacity
    stored_total, rank_width = adapter_down_store.shape[0], adapter_down_store.shape[1]
    adapter_count = adapter_store_row.shape[0]

    if key_cache_table.shape[2] == HEAD_WIDTH and requests % BLOCK_REQUESTS == 0:
        attended = attention_blocked(queries, key_cache_table, value_cache_table, filled_lengths)
    else:
        attended = attention(queries, key_cache_table, value_cache_table, filled_lengths)

    own_ids = lax.dynamic_slice_in_dim(request_adapter, group_index * requests, requests)
    id_hot = own_ids[:, None] == jnp.arange(adapter_count)[None, :]
    own_row = jnp.sum(jnp.where(id_hot, adapter_store_row[None, :], 0), axis=1)
    own_dest = own_row // stored_total
    same_dest = own_dest[:, None] == own_dest[None, :]
    before = jnp.arange(requests)[:, None] > jnp.arange(requests)[None, :]
    own_order = jnp.sum((same_dest & before).astype(jnp.int32), axis=1)
    own_cell = own_dest * capacity + own_order
    cell_hot = own_cell[None, :] == jnp.arange(slot_count)[:, None]
    outgoing = jnp.einsum(
        "cb,bf->cf", cell_hot.astype(jnp.bfloat16), attended, preferred_element_type=jnp.float32
    ).astype(jnp.bfloat16)
    arrived = lax.all_to_all(
        outgoing.reshape(group_count, capacity, row_width), "dp", 0, 0, tiled=True
    ).reshape(slot_count, row_width)

    local_rows = group_index * stored_total + jnp.arange(stored_total)
    holds = adapter_store_row[None, :] == local_rows[:, None]
    local_ids = jnp.sum(jnp.where(holds, jnp.arange(adapter_count)[None, :], 0), axis=1)
    local_factor = jnp.sum(jnp.where(holds, adapter_factor[None, :], 0.0), axis=1)
    all_ids = request_adapter.reshape(group_count, requests)
    hit = (all_ids[:, :, None] == local_ids[None, None, :]).astype(jnp.bfloat16)
    mine = jnp.sum(hit, axis=2)
    order_in = prefix_count(mine)
    pick = (mine[:, None, :] > 0) & (
        order_in[:, None, :] == jnp.arange(capacity, dtype=jnp.float32)[None, :, None]
    )
    picked = jnp.einsum(
        "gcb,gbj->gcj", pick.astype(jnp.bfloat16), hit, preferred_element_type=jnp.float32
    ).reshape(slot_count, stored_total)
    item_scale = jnp.dot(picked, local_factor, precision=lax.Precision.HIGHEST)

    store_down = adapter_down_store.reshape(stored_total * rank_width, row_width)
    products = lax.dot_general(
        arrived, store_down, (((1,), (1,)), ((), ())), preferred_element_type=jnp.float32
    )
    partial_value = jnp.sum(
        products.reshape(slot_count, stored_total, rank_width) * picked[:, :, None], axis=1
    )
    summed = of_everyone(partial_value, "tensor")
    low_rank = (summed * item_scale[:, None]).astype(jnp.bfloat16)
    spread = (picked.astype(jnp.bfloat16)[:, :, None] * low_rank[:, None, :]).reshape(
        slot_count, stored_total * rank_width
    )
    store_up = adapter_up_store.reshape(stored_total * rank_width, row_width)
    result = jnp.dot(spread, store_up, preferred_element_type=jnp.float32).astype(jnp.bfloat16)
    returned = lax.all_to_all(
        result.reshape(group_count, capacity, row_width), "dp", 0, 0, tiled=True
    ).reshape(slot_count, row_width)
    adapter_delta = jnp.einsum(
        "cb,cf->bf", cell_hot.astype(jnp.bfloat16), returned, preferred_element_type=jnp.float32
    ).astype(jnp.bfloat16)
    return (attended, adapter_delta)


def solution(mesh):
    placed = (
        P("dp", "tensor"),
        P("dp", None, "tensor"),
        P("dp", None, "tensor"),
        P("dp"),
        P(),
        P(),
        P(),
        P("dp", None, "tensor"),
        P("dp", None, "tensor"),
    )
    return jax.shard_map(
        body,
        mesh=mesh,
        in_specs=placed,
        out_specs=(P("dp", "tensor"), P("dp", "tensor")),
        check_vma=False,
    )
```

```python
import math

import jax
import jax.numpy as jnp
from jax import lax
from jax.sharding import PartitionSpec as P

HEAD_WIDTH = 128
BLOCK_REQUESTS = 4


def of_everyone(value, axis):
    copies = jnp.broadcast_to(value, (lax.axis_size(axis), *value.shape))
    return lax.all_to_all(copies, axis, split_axis=0, concat_axis=0, tiled=True).sum(axis=0)


def attention(queries, key_cache_table, value_cache_table, filled_lengths):
    requests, row_width = queries.shape
    kv_local = key_cache_table.shape[2] // HEAD_WIDTH
    group_width = row_width // HEAD_WIDTH // kv_local
    length = key_cache_table.shape[1]
    heads_of_query = queries.reshape(requests, kv_local, group_width, HEAD_WIDTH)
    heads_of_key = key_cache_table.reshape(requests, length, kv_local, HEAD_WIDTH)
    heads_of_value = value_cache_table.reshape(requests, length, kv_local, HEAD_WIDTH)
    scores = jnp.einsum(
        "bkgd,blkd->bkgl", heads_of_query, heads_of_key, preferred_element_type=jnp.float32
    ) * (1.0 / math.sqrt(HEAD_WIDTH))
    visible = (jnp.arange(length)[None, :] < filled_lengths[:, None])[:, None, None, :]
    scores = jnp.where(visible, scores, jnp.float32(-1e30))
    row_max = jnp.max(scores, axis=-1, keepdims=True)
    exp_scores = jnp.exp(scores - row_max)
    weights = (exp_scores / jnp.sum(exp_scores, axis=-1, keepdims=True)).astype(jnp.bfloat16)
    attended = jnp.einsum(
        "bkgl,blkd->bkgd", weights, heads_of_value, preferred_element_type=jnp.float32
    )
    return attended.astype(jnp.bfloat16).reshape(requests, row_width)


def attention_blocked(queries, key_cache_table, value_cache_table, filled_lengths):
    requests, row_width = queries.shape
    heads = row_width // HEAD_WIDTH
    length = key_cache_table.shape[1]
    block = BLOCK_REQUESTS
    count = requests // block
    stacked = (
        queries.reshape(count, block, heads, HEAD_WIDTH)
        .transpose(0, 2, 1, 3)
        .reshape(count, heads * block, HEAD_WIDTH)
    )
    keys = key_cache_table.reshape(count, block * length, HEAD_WIDTH)
    values = value_cache_table.reshape(count, block * length, HEAD_WIDTH)
    scores = jnp.einsum(
        "nrd,njd->nrj", stacked, keys, preferred_element_type=jnp.float32
    ) * (1.0 / math.sqrt(HEAD_WIDTH))
    row_request = jnp.arange(heads * block) % block
    col_request = jnp.arange(block * length) // length
    col_slot = jnp.arange(block * length) % length
    col_length = jnp.repeat(filled_lengths.reshape(count, block), length, axis=1)
    visible = (row_request[:, None] == col_request[None, :])[None] & (
        col_slot[None, None, :] < col_length[:, None, :]
    )
    scores = jnp.where(visible, scores, jnp.float32(-1e30))
    row_max = jnp.max(scores, axis=-1, keepdims=True)
    exp_scores = jnp.exp(scores - row_max)
    weights = (exp_scores / jnp.sum(exp_scores, axis=-1, keepdims=True)).astype(jnp.bfloat16)
    weights = lax.optimization_barrier(weights)
    attended = jnp.einsum("nrj,njd->nrd", weights, values, preferred_element_type=jnp.float32)
    return (
        attended.astype(jnp.bfloat16)
        .reshape(count, heads, block, HEAD_WIDTH)
        .transpose(0, 2, 1, 3)
        .reshape(requests, row_width)
    )


def prefix_count(mask):
    n = mask.shape[-1]
    earlier = (jnp.arange(n)[:, None] < jnp.arange(n)[None, :]).astype(jnp.bfloat16)
    return jnp.einsum(
        "...i,ij->...j", mask.astype(jnp.bfloat16), earlier, preferred_element_type=jnp.float32
    )


def body(
    queries,
    key_cache_table,
    value_cache_table,
    filled_lengths,
    request_adapter,
    adapter_store_row,
    adapter_factor,
    adapter_down_store,
    adapter_up_store,
):
    requests, row_width = queries.shape
    group_count = lax.axis_size("dp")
    group_index = lax.axis_index("dp")
    capacity = max(2, 2 * requests // group_count)
    slot_count = group_count * capacity
    stored_total, rank_width = adapter_down_store.shape[0], adapter_down_store.shape[1]
    adapter_count = adapter_store_row.shape[0]

    if key_cache_table.shape[2] == HEAD_WIDTH and requests % BLOCK_REQUESTS == 0:
        attended = attention_blocked(queries, key_cache_table, value_cache_table, filled_lengths)
    else:
        attended = attention(queries, key_cache_table, value_cache_table, filled_lengths)

    own_ids = lax.dynamic_slice_in_dim(request_adapter, group_index * requests, requests)
    id_hot = own_ids[:, None] == jnp.arange(adapter_count)[None, :]
    own_row = jnp.sum(jnp.where(id_hot, adapter_store_row[None, :], 0), axis=1)
    own_dest = own_row // stored_total
    same_dest = own_dest[:, None] == own_dest[None, :]
    before = jnp.arange(requests)[:, None] > jnp.arange(requests)[None, :]
    own_order = jnp.sum((same_dest & before).astype(jnp.int32), axis=1)
    own_cell = own_dest * capacity + own_order
    cell_hot = lax.optimization_barrier(
        (own_cell[None, :] == jnp.arange(slot_count)[:, None]).astype(jnp.bfloat16)
    )
    outgoing = jnp.einsum(
        "cb,bf->cf", cell_hot, attended, preferred_element_type=jnp.float32
    ).astype(jnp.bfloat16)
    arrived = lax.all_to_all(
        outgoing.reshape(group_count, capacity, row_width), "dp", 0, 0, tiled=True
    ).reshape(slot_count, row_width)

    local_rows = group_index * stored_total + jnp.arange(stored_total)
    holds = adapter_store_row[None, :] == local_rows[:, None]
    local_ids = jnp.sum(jnp.where(holds, jnp.arange(adapter_count)[None, :], 0), axis=1)
    local_factor = jnp.sum(jnp.where(holds, adapter_factor[None, :], 0.0), axis=1)
    all_ids = request_adapter.reshape(group_count, requests)
    hit = (all_ids[:, :, None] == local_ids[None, None, :]).astype(jnp.bfloat16)
    mine = jnp.sum(hit, axis=2)
    order_in = prefix_count(mine)
    pick = (mine[:, None, :] > 0) & (
        order_in[:, None, :] == jnp.arange(capacity, dtype=jnp.float32)[None, :, None]
    )
    picked = jnp.einsum(
        "gcb,gbj->gcj", pick.astype(jnp.bfloat16), hit, preferred_element_type=jnp.float32
    ).reshape(slot_count, stored_total)
    item_scale = jnp.dot(picked, local_factor, precision=lax.Precision.HIGHEST)

    store_down = adapter_down_store.reshape(stored_total * rank_width, row_width)
    products = lax.dot_general(
        arrived, store_down, (((1,), (1,)), ((), ())), preferred_element_type=jnp.float32
    )
    partial_value = jnp.sum(
        products.reshape(slot_count, stored_total, rank_width) * picked[:, :, None], axis=1
    )
    summed = of_everyone(partial_value, "tensor")
    low_rank = (summed * item_scale[:, None]).astype(jnp.bfloat16)
    spread = (picked.astype(jnp.bfloat16)[:, :, None] * low_rank[:, None, :]).reshape(
        slot_count, stored_total * rank_width
    )
    store_up = adapter_up_store.reshape(stored_total * rank_width, row_width)
    result = jnp.dot(spread, store_up, preferred_element_type=jnp.float32).astype(jnp.bfloat16)
    returned = lax.all_to_all(
        result.reshape(group_count, capacity, row_width), "dp", 0, 0, tiled=True
    ).reshape(slot_count, row_width)
    adapter_delta = jnp.einsum(
        "cb,cf->bf", cell_hot, returned, preferred_element_type=jnp.float32
    ).astype(jnp.bfloat16)
    return (attended, adapter_delta)


def solution(mesh):
    placed = (
        P("dp", "tensor"),
        P("dp", None, "tensor"),
        P("dp", None, "tensor"),
        P("dp"),
        P(),
        P(),
        P(),
        P("dp", None, "tensor"),
        P("dp", None, "tensor"),
    )
    return jax.shard_map(
        body,
        mesh=mesh,
        in_specs=placed,
        out_specs=(P("dp", "tensor"), P("dp", "tensor")),
        check_vma=False,
    )
```

```python
import math

import jax
import jax.numpy as jnp
from jax import lax
from jax.sharding import PartitionSpec as P

HEAD_WIDTH = 128
BLOCK_REQUESTS = 4


def of_everyone(value, axis):
    copies = jnp.broadcast_to(value, (lax.axis_size(axis), *value.shape))
    return lax.all_to_all(copies, axis, split_axis=0, concat_axis=0, tiled=True).sum(axis=0)


def attention(queries, key_cache_table, value_cache_table, filled_lengths):
    requests, row_width = queries.shape
    kv_local = key_cache_table.shape[2] // HEAD_WIDTH
    group_width = row_width // HEAD_WIDTH // kv_local
    length = key_cache_table.shape[1]
    heads_of_query = queries.reshape(requests, kv_local, group_width, HEAD_WIDTH)
    heads_of_key = key_cache_table.reshape(requests, length, kv_local, HEAD_WIDTH)
    heads_of_value = value_cache_table.reshape(requests, length, kv_local, HEAD_WIDTH)
    scores = jnp.einsum(
        "bkgd,blkd->bkgl", heads_of_query, heads_of_key, preferred_element_type=jnp.float32
    ) * (1.0 / math.sqrt(HEAD_WIDTH))
    visible = (jnp.arange(length)[None, :] < filled_lengths[:, None])[:, None, None, :]
    scores = jnp.where(visible, scores, jnp.float32(-1e30))
    row_max = jnp.max(scores, axis=-1, keepdims=True)
    exp_scores = jnp.exp(scores - row_max)
    weights = (exp_scores / jnp.sum(exp_scores, axis=-1, keepdims=True)).astype(jnp.bfloat16)
    attended = jnp.einsum(
        "bkgl,blkd->bkgd", weights, heads_of_value, preferred_element_type=jnp.float32
    )
    return attended.astype(jnp.bfloat16).reshape(requests, row_width)


def attention_blocked(queries, key_cache_table, value_cache_table, filled_lengths):
    requests, row_width = queries.shape
    heads = row_width // HEAD_WIDTH
    length = key_cache_table.shape[1]
    block = BLOCK_REQUESTS
    count = requests // block
    stacked = (
        queries.reshape(count, block, heads, HEAD_WIDTH)
        .transpose(0, 2, 1, 3)
        .reshape(count, heads * block, HEAD_WIDTH)
    )
    keys = key_cache_table.reshape(count, block * length, HEAD_WIDTH)
    values = value_cache_table.reshape(count, block * length, HEAD_WIDTH)
    scores = jnp.einsum(
        "nrd,njd->nrj", stacked, keys, preferred_element_type=jnp.float32
    ) * (1.0 / math.sqrt(HEAD_WIDTH))
    row_request = jnp.arange(heads * block) % block
    col_request = jnp.arange(block * length) // length
    col_slot = jnp.arange(block * length) % length
    col_length = jnp.repeat(filled_lengths.reshape(count, block), length, axis=1)
    visible = (row_request[:, None] == col_request[None, :])[None] & (
        col_slot[None, None, :] < col_length[:, None, :]
    )
    scores = jnp.where(visible, scores, jnp.float32(-1e30))
    row_max = jnp.max(scores, axis=-1, keepdims=True)
    exp_scores = jnp.exp(scores - row_max)
    weights = (exp_scores / jnp.sum(exp_scores, axis=-1, keepdims=True)).astype(jnp.bfloat16)
    weights = lax.optimization_barrier(weights)
    attended = jnp.einsum("nrj,njd->nrd", weights, values, preferred_element_type=jnp.float32)
    return (
        attended.astype(jnp.bfloat16)
        .reshape(count, heads, block, HEAD_WIDTH)
        .transpose(0, 2, 1, 3)
        .reshape(requests, row_width)
    )


def prefix_count(mask):
    n = mask.shape[-1]
    earlier = (jnp.arange(n)[:, None] < jnp.arange(n)[None, :]).astype(jnp.bfloat16)
    return jnp.einsum(
        "...i,ij->...j", mask.astype(jnp.bfloat16), earlier, preferred_element_type=jnp.float32
    )


def body(
    queries,
    key_cache_table,
    value_cache_table,
    filled_lengths,
    request_adapter,
    adapter_store_row,
    adapter_factor,
    adapter_down_store,
    adapter_up_store,
):
    requests, row_width = queries.shape
    group_count = lax.axis_size("dp")
    group_index = lax.axis_index("dp")
    capacity = max(2, 2 * requests // group_count)
    slot_count = group_count * capacity
    stored_total, rank_width = adapter_down_store.shape[0], adapter_down_store.shape[1]
    adapter_count = adapter_store_row.shape[0]

    if key_cache_table.shape[2] == HEAD_WIDTH and requests % BLOCK_REQUESTS == 0:
        attended = attention_blocked(queries, key_cache_table, value_cache_table, filled_lengths)
    else:
        attended = attention(queries, key_cache_table, value_cache_table, filled_lengths)

    own_ids = lax.dynamic_slice_in_dim(request_adapter, group_index * requests, requests)
    id_hot = own_ids[:, None] == jnp.arange(adapter_count)[None, :]
    own_row = jnp.sum(jnp.where(id_hot, adapter_store_row[None, :], 0), axis=1)
    own_dest = own_row // stored_total
    same_dest = own_dest[:, None] == own_dest[None, :]
    before = jnp.arange(requests)[:, None] > jnp.arange(requests)[None, :]
    own_order = jnp.sum((same_dest & before).astype(jnp.int32), axis=1)
    own_cell = own_dest * capacity + own_order
    cell_hot, request_hot = lax.optimization_barrier(
        (
            (own_cell[None, :] == jnp.arange(slot_count)[:, None]).astype(jnp.bfloat16),
            (own_cell[:, None] == jnp.arange(slot_count)[None, :]).astype(jnp.bfloat16),
        )
    )
    outgoing = jnp.einsum(
        "cb,bf->cf", cell_hot, attended, preferred_element_type=jnp.float32
    ).astype(jnp.bfloat16)
    arrived = lax.all_to_all(
        outgoing.reshape(group_count, capacity, row_width), "dp", 0, 0, tiled=True
    ).reshape(slot_count, row_width)

    local_rows = group_index * stored_total + jnp.arange(stored_total)
    holds = adapter_store_row[None, :] == local_rows[:, None]
    local_ids = jnp.sum(jnp.where(holds, jnp.arange(adapter_count)[None, :], 0), axis=1)
    local_factor = jnp.sum(jnp.where(holds, adapter_factor[None, :], 0.0), axis=1)
    all_ids = request_adapter.reshape(group_count, requests)
    hit = (all_ids[:, :, None] == local_ids[None, None, :]).astype(jnp.bfloat16)
    mine = jnp.sum(hit, axis=2)
    order_in = prefix_count(mine)
    pick = (mine[:, None, :] > 0) & (
        order_in[:, None, :] == jnp.arange(capacity, dtype=jnp.float32)[None, :, None]
    )
    picked = jnp.einsum(
        "gcb,gbj->gcj", pick.astype(jnp.bfloat16), hit, preferred_element_type=jnp.float32
    ).reshape(slot_count, stored_total)
    item_scale = jnp.dot(picked, local_factor, precision=lax.Precision.HIGHEST)

    store_down = adapter_down_store.reshape(stored_total * rank_width, row_width)
    products = lax.dot_general(
        arrived, store_down, (((1,), (1,)), ((), ())), preferred_element_type=jnp.float32
    )
    partial_value = jnp.sum(
        products.reshape(slot_count, stored_total, rank_width) * picked[:, :, None], axis=1
    )
    summed = of_everyone(partial_value, "tensor")
    low_rank = (summed * item_scale[:, None]).astype(jnp.bfloat16)
    spread = (picked.astype(jnp.bfloat16)[:, :, None] * low_rank[:, None, :]).reshape(
        slot_count, stored_total * rank_width
    )
    store_up = adapter_up_store.reshape(stored_total * rank_width, row_width)
    result = jnp.dot(spread, store_up, preferred_element_type=jnp.float32).astype(jnp.bfloat16)
    returned = lax.all_to_all(
        result.reshape(group_count, capacity, row_width), "dp", 0, 0, tiled=True
    ).reshape(slot_count, row_width)
    adapter_delta = jnp.dot(request_hot, returned, preferred_element_type=jnp.float32).astype(
        jnp.bfloat16
    )
    return (attended, adapter_delta)


def solution(mesh):
    placed = (
        P("dp", "tensor"),
        P("dp", None, "tensor"),
        P("dp", None, "tensor"),
        P("dp"),
        P(),
        P(),
        P(),
        P("dp", None, "tensor"),
        P("dp", None, "tensor"),
    )
    return jax.shard_map(
        body,
        mesh=mesh,
        in_specs=placed,
        out_specs=(P("dp", "tensor"), P("dp", "tensor")),
        check_vma=False,
    )
```

```python
import math

import jax
import jax.numpy as jnp
from jax import lax
from jax.sharding import PartitionSpec as P

HEAD_WIDTH = 128
BLOCK_REQUESTS = 4


def of_everyone(value, axis):
    copies = jnp.broadcast_to(value, (lax.axis_size(axis), *value.shape))
    return lax.all_to_all(copies, axis, split_axis=0, concat_axis=0, tiled=True).sum(axis=0)


def attention(queries, key_cache_table, value_cache_table, filled_lengths):
    requests, row_width = queries.shape
    kv_local = key_cache_table.shape[2] // HEAD_WIDTH
    group_width = row_width // HEAD_WIDTH // kv_local
    length = key_cache_table.shape[1]
    heads_of_query = queries.reshape(requests, kv_local, group_width, HEAD_WIDTH)
    heads_of_key = key_cache_table.reshape(requests, length, kv_local, HEAD_WIDTH)
    heads_of_value = value_cache_table.reshape(requests, length, kv_local, HEAD_WIDTH)
    scores = jnp.einsum(
        "bkgd,blkd->bkgl", heads_of_query, heads_of_key, preferred_element_type=jnp.float32
    ) * (1.0 / math.sqrt(HEAD_WIDTH))
    visible = (jnp.arange(length)[None, :] < filled_lengths[:, None])[:, None, None, :]
    scores = jnp.where(visible, scores, jnp.float32(-1e30))
    row_max = jnp.max(scores, axis=-1, keepdims=True)
    exp_scores = jnp.exp(scores - row_max)
    weights = (exp_scores / jnp.sum(exp_scores, axis=-1, keepdims=True)).astype(jnp.bfloat16)
    attended = jnp.einsum(
        "bkgl,blkd->bkgd", weights, heads_of_value, preferred_element_type=jnp.float32
    )
    return attended.astype(jnp.bfloat16).reshape(requests, row_width)


def attention_blocked(queries, key_cache_table, value_cache_table, filled_lengths):
    requests, row_width = queries.shape
    heads = row_width // HEAD_WIDTH
    length = key_cache_table.shape[1]
    block = BLOCK_REQUESTS
    count = requests // block
    stacked = (
        queries.reshape(count, block, heads, HEAD_WIDTH)
        .transpose(0, 2, 1, 3)
        .reshape(count, heads * block, HEAD_WIDTH)
    )
    keys = key_cache_table.reshape(count, block * length, HEAD_WIDTH)
    values = value_cache_table.reshape(count, block * length, HEAD_WIDTH)
    scores = jnp.einsum(
        "nrd,njd->nrj", stacked, keys, preferred_element_type=jnp.float32
    ) * (1.0 / math.sqrt(HEAD_WIDTH))
    row_request = jnp.arange(heads * block) % block
    col_request = jnp.arange(block * length) // length
    col_slot = jnp.arange(block * length) % length
    col_index = (
        jnp.arange(count)[:, None] * block + jnp.arange(block * length)[None, :] // length
    )
    col_length = jnp.take(filled_lengths, col_index, mode="clip")
    visible = (row_request[:, None] == col_request[None, :])[None] & (
        col_slot[None, None, :] < col_length[:, None, :]
    )
    scores = jnp.where(visible, scores, jnp.float32(-1e30))
    row_max = jnp.max(scores, axis=-1, keepdims=True)
    exp_scores = jnp.exp(scores - row_max)
    weights = (exp_scores / jnp.sum(exp_scores, axis=-1, keepdims=True)).astype(jnp.bfloat16)
    weights = lax.optimization_barrier(weights)
    attended = jnp.einsum("nrj,njd->nrd", weights, values, preferred_element_type=jnp.float32)
    return (
        attended.astype(jnp.bfloat16)
        .reshape(count, heads, block, HEAD_WIDTH)
        .transpose(0, 2, 1, 3)
        .reshape(requests, row_width)
    )


def prefix_count(mask):
    n = mask.shape[-1]
    earlier = (jnp.arange(n)[:, None] < jnp.arange(n)[None, :]).astype(jnp.bfloat16)
    return jnp.einsum(
        "...i,ij->...j", mask.astype(jnp.bfloat16), earlier, preferred_element_type=jnp.float32
    )


def body(
    queries,
    key_cache_table,
    value_cache_table,
    filled_lengths,
    request_adapter,
    adapter_store_row,
    adapter_factor,
    adapter_down_store,
    adapter_up_store,
):
    requests, row_width = queries.shape
    group_count = lax.axis_size("dp")
    group_index = lax.axis_index("dp")
    capacity = max(2, 2 * requests // group_count)
    slot_count = group_count * capacity
    stored_total, rank_width = adapter_down_store.shape[0], adapter_down_store.shape[1]
    adapter_count = adapter_store_row.shape[0]

    if key_cache_table.shape[2] == HEAD_WIDTH and requests % BLOCK_REQUESTS == 0:
        attended = attention_blocked(queries, key_cache_table, value_cache_table, filled_lengths)
    else:
        attended = attention(queries, key_cache_table, value_cache_table, filled_lengths)

    own_ids = lax.dynamic_slice_in_dim(request_adapter, group_index * requests, requests)
    id_hot = own_ids[:, None] == jnp.arange(adapter_count)[None, :]
    own_row = jnp.sum(jnp.where(id_hot, adapter_store_row[None, :], 0), axis=1)
    own_dest = own_row // stored_total
    same_dest = own_dest[:, None] == own_dest[None, :]
    before = jnp.arange(requests)[:, None] > jnp.arange(requests)[None, :]
    own_order = jnp.sum((same_dest & before).astype(jnp.int32), axis=1)
    own_cell = own_dest * capacity + own_order
    cell_hot = lax.optimization_barrier(
        (own_cell[None, :] == jnp.arange(slot_count)[:, None]).astype(jnp.bfloat16)
    )
    outgoing = jnp.einsum(
        "cb,bf->cf", cell_hot, attended, preferred_element_type=jnp.float32
    ).astype(jnp.bfloat16)
    arrived = lax.all_to_all(
        outgoing.reshape(group_count, capacity, row_width), "dp", 0, 0, tiled=True
    ).reshape(slot_count, row_width)

    local_rows = group_index * stored_total + jnp.arange(stored_total)
    holds = adapter_store_row[None, :] == local_rows[:, None]
    local_ids = jnp.sum(jnp.where(holds, jnp.arange(adapter_count)[None, :], 0), axis=1)
    local_factor = jnp.sum(jnp.where(holds, adapter_factor[None, :], 0.0), axis=1)
    all_ids = request_adapter.reshape(group_count, requests)
    hit = (all_ids[:, :, None] == local_ids[None, None, :]).astype(jnp.bfloat16)
    mine = jnp.sum(hit, axis=2)
    order_in = prefix_count(mine)
    pick = (mine[:, None, :] > 0) & (
        order_in[:, None, :] == jnp.arange(capacity, dtype=jnp.float32)[None, :, None]
    )
    picked = jnp.einsum(
        "gcb,gbj->gcj", pick.astype(jnp.bfloat16), hit, preferred_element_type=jnp.float32
    ).reshape(slot_count, stored_total)
    item_scale = jnp.dot(picked, local_factor, precision=lax.Precision.HIGHEST)

    store_down = adapter_down_store.reshape(stored_total * rank_width, row_width)
    products = lax.dot_general(
        arrived, store_down, (((1,), (1,)), ((), ())), preferred_element_type=jnp.float32
    )
    partial_value = jnp.sum(
        products.reshape(slot_count, stored_total, rank_width) * picked[:, :, None], axis=1
    )
    summed = of_everyone(partial_value, "tensor")
    low_rank = (summed * item_scale[:, None]).astype(jnp.bfloat16)
    spread = (picked.astype(jnp.bfloat16)[:, :, None] * low_rank[:, None, :]).reshape(
        slot_count, stored_total * rank_width
    )
    store_up = adapter_up_store.reshape(stored_total * rank_width, row_width)
    result = jnp.dot(spread, store_up, preferred_element_type=jnp.float32).astype(jnp.bfloat16)
    returned = lax.all_to_all(
        result.reshape(group_count, capacity, row_width), "dp", 0, 0, tiled=True
    ).reshape(slot_count, row_width)
    adapter_delta = jnp.einsum(
        "cb,cf->bf", cell_hot, returned, preferred_element_type=jnp.float32
    ).astype(jnp.bfloat16)
    return (attended, adapter_delta)


def solution(mesh):
    placed = (
        P("dp", "tensor"),
        P("dp", None, "tensor"),
        P("dp", None, "tensor"),
        P("dp"),
        P(),
        P(),
        P(),
        P("dp", None, "tensor"),
        P("dp", None, "tensor"),
    )
    return jax.shard_map(
        body,
        mesh=mesh,
        in_specs=placed,
        out_specs=(P("dp", "tensor"), P("dp", "tensor")),
        check_vma=False,
    )
```

```python
import math

import jax
import jax.numpy as jnp
from jax import lax
from jax.sharding import PartitionSpec as P

HEAD_WIDTH = 128
BLOCK_REQUESTS = 4


def of_everyone(value, axis):
    copies = jnp.broadcast_to(value, (lax.axis_size(axis), *value.shape))
    return lax.all_to_all(copies, axis, split_axis=0, concat_axis=0, tiled=True).sum(axis=0)


def attention(queries, key_cache_table, value_cache_table, filled_lengths):
    requests, row_width = queries.shape
    kv_local = key_cache_table.shape[2] // HEAD_WIDTH
    group_width = row_width // HEAD_WIDTH // kv_local
    length = key_cache_table.shape[1]
    heads_of_query = queries.reshape(requests, kv_local, group_width, HEAD_WIDTH)
    heads_of_key = key_cache_table.reshape(requests, length, kv_local, HEAD_WIDTH)
    heads_of_value = value_cache_table.reshape(requests, length, kv_local, HEAD_WIDTH)
    scores = jnp.einsum(
        "bkgd,blkd->bkgl", heads_of_query, heads_of_key, preferred_element_type=jnp.float32
    ) * (1.0 / math.sqrt(HEAD_WIDTH))
    visible = (jnp.arange(length)[None, :] < filled_lengths[:, None])[:, None, None, :]
    scores = jnp.where(visible, scores, jnp.float32(-1e30))
    row_max = jnp.max(scores, axis=-1, keepdims=True)
    exp_scores = jnp.exp(scores - row_max)
    weights = (exp_scores / jnp.sum(exp_scores, axis=-1, keepdims=True)).astype(jnp.bfloat16)
    attended = jnp.einsum(
        "bkgl,blkd->bkgd", weights, heads_of_value, preferred_element_type=jnp.float32
    )
    return attended.astype(jnp.bfloat16).reshape(requests, row_width)


def attention_blocked(queries, key_cache_table, value_cache_table, filled_lengths):
    requests, row_width = queries.shape
    heads = row_width // HEAD_WIDTH
    length = key_cache_table.shape[1]
    block = BLOCK_REQUESTS
    count = requests // block
    stacked = (
        queries.reshape(count, block, heads, HEAD_WIDTH)
        .transpose(0, 2, 1, 3)
        .reshape(count, heads * block, HEAD_WIDTH)
    )
    keys = key_cache_table.reshape(count, block * length, HEAD_WIDTH)
    values = value_cache_table.reshape(count, block * length, HEAD_WIDTH)
    scores = jnp.einsum(
        "nrd,njd->nrj", stacked, keys, preferred_element_type=jnp.float32
    ) * (1.0 / math.sqrt(HEAD_WIDTH))
    row_request = jnp.arange(heads * block) % block
    col_request = jnp.arange(block * length) // length
    col_slot = jnp.arange(block * length) % length
    col_length = jnp.repeat(filled_lengths.reshape(count, block), length, axis=1)
    visible = (row_request[:, None] == col_request[None, :])[None] & (
        col_slot[None, None, :] < col_length[:, None, :]
    )
    scores = jnp.where(visible, scores, jnp.float32(-1e30))
    row_max = jnp.max(scores, axis=-1, keepdims=True)
    exp_scores = jnp.exp(scores - row_max)
    weights = (exp_scores / jnp.sum(exp_scores, axis=-1, keepdims=True)).astype(jnp.bfloat16)
    weights = lax.optimization_barrier(weights)
    attended = jnp.einsum("nrj,njd->nrd", weights, values, preferred_element_type=jnp.float32)
    return (
        attended.astype(jnp.bfloat16)
        .reshape(count, heads, block, HEAD_WIDTH)
        .transpose(0, 2, 1, 3)
        .reshape(requests, row_width)
    )


def prefix_count(mask):
    n = mask.shape[-1]
    earlier = (jnp.arange(n)[:, None] < jnp.arange(n)[None, :]).astype(jnp.bfloat16)
    return jnp.einsum(
        "...i,ij->...j", mask.astype(jnp.bfloat16), earlier, preferred_element_type=jnp.float32
    )


def body(
    queries,
    key_cache_table,
    value_cache_table,
    filled_lengths,
    request_adapter,
    adapter_store_row,
    adapter_factor,
    adapter_down_store,
    adapter_up_store,
):
    requests, row_width = queries.shape
    group_count = lax.axis_size("dp")
    group_index = lax.axis_index("dp")
    capacity = max(2, 2 * requests // group_count)
    slot_count = group_count * capacity
    stored_total, rank_width = adapter_down_store.shape[0], adapter_down_store.shape[1]
    adapter_count = adapter_store_row.shape[0]

    if key_cache_table.shape[2] == HEAD_WIDTH and requests % BLOCK_REQUESTS == 0:
        attended = attention_blocked(queries, key_cache_table, value_cache_table, filled_lengths)
    else:
        attended = attention(queries, key_cache_table, value_cache_table, filled_lengths)

    own_ids = lax.dynamic_slice_in_dim(request_adapter, group_index * requests, requests)
    own_row = jnp.take(adapter_store_row, own_ids, mode="clip")
    own_dest = own_row // stored_total
    same_dest = own_dest[:, None] == own_dest[None, :]
    before = jnp.arange(requests)[:, None] > jnp.arange(requests)[None, :]
    own_order = jnp.sum((same_dest & before).astype(jnp.int32), axis=1)
    own_cell = own_dest * capacity + own_order
    cell_hot = lax.optimization_barrier(
        (own_cell[None, :] == jnp.arange(slot_count)[:, None]).astype(jnp.bfloat16)
    )
    outgoing = jnp.einsum(
        "cb,bf->cf", cell_hot, attended, preferred_element_type=jnp.float32
    ).astype(jnp.bfloat16)
    arrived = lax.all_to_all(
        outgoing.reshape(group_count, capacity, row_width), "dp", 0, 0, tiled=True
    ).reshape(slot_count, row_width)

    local_rows = group_index * stored_total + jnp.arange(stored_total)
    holds = adapter_store_row[None, :] == local_rows[:, None]
    local_ids = jnp.sum(jnp.where(holds, jnp.arange(adapter_count)[None, :], 0), axis=1)
    local_factor = jnp.sum(jnp.where(holds, adapter_factor[None, :], 0.0), axis=1)
    all_ids = request_adapter.reshape(group_count, requests)
    hit = (all_ids[:, :, None] == local_ids[None, None, :]).astype(jnp.bfloat16)
    mine = jnp.sum(hit, axis=2)
    order_in = prefix_count(mine)
    pick = (mine[:, None, :] > 0) & (
        order_in[:, None, :] == jnp.arange(capacity, dtype=jnp.float32)[None, :, None]
    )
    picked = jnp.einsum(
        "gcb,gbj->gcj", pick.astype(jnp.bfloat16), hit, preferred_element_type=jnp.float32
    ).reshape(slot_count, stored_total)
    item_scale = jnp.dot(picked, local_factor, precision=lax.Precision.HIGHEST)

    store_down = adapter_down_store.reshape(stored_total * rank_width, row_width)
    products = lax.dot_general(
        arrived, store_down, (((1,), (1,)), ((), ())), preferred_element_type=jnp.float32
    )
    partial_value = jnp.sum(
        products.reshape(slot_count, stored_total, rank_width) * picked[:, :, None], axis=1
    )
    summed = of_everyone(partial_value, "tensor")
    low_rank = (summed * item_scale[:, None]).astype(jnp.bfloat16)
    spread = (picked.astype(jnp.bfloat16)[:, :, None] * low_rank[:, None, :]).reshape(
        slot_count, stored_total * rank_width
    )
    store_up = adapter_up_store.reshape(stored_total * rank_width, row_width)
    result = jnp.dot(spread, store_up, preferred_element_type=jnp.float32).astype(jnp.bfloat16)
    returned = lax.all_to_all(
        result.reshape(group_count, capacity, row_width), "dp", 0, 0, tiled=True
    ).reshape(slot_count, row_width)
    adapter_delta = jnp.einsum(
        "cb,cf->bf", cell_hot, returned, preferred_element_type=jnp.float32
    ).astype(jnp.bfloat16)
    return (attended, adapter_delta)


def solution(mesh):
    placed = (
        P("dp", "tensor"),
        P("dp", None, "tensor"),
        P("dp", None, "tensor"),
        P("dp"),
        P(),
        P(),
        P(),
        P("dp", None, "tensor"),
        P("dp", None, "tensor"),
    )
    return jax.shard_map(
        body,
        mesh=mesh,
        in_specs=placed,
        out_specs=(P("dp", "tensor"), P("dp", "tensor")),
        check_vma=False,
    )
```

```python
import math

import jax
import jax.numpy as jnp
from jax import lax
from jax.sharding import PartitionSpec as P

HEAD_WIDTH = 128
BLOCK_REQUESTS = 4


def of_everyone(value, axis):
    copies = jnp.broadcast_to(value, (lax.axis_size(axis), *value.shape))
    return lax.all_to_all(copies, axis, split_axis=0, concat_axis=0, tiled=True).sum(axis=0)


def attention(queries, key_cache_table, value_cache_table, filled_lengths):
    requests, row_width = queries.shape
    kv_local = key_cache_table.shape[2] // HEAD_WIDTH
    group_width = row_width // HEAD_WIDTH // kv_local
    length = key_cache_table.shape[1]
    heads_of_query = queries.reshape(requests, kv_local, group_width, HEAD_WIDTH)
    heads_of_key = key_cache_table.reshape(requests, length, kv_local, HEAD_WIDTH)
    heads_of_value = value_cache_table.reshape(requests, length, kv_local, HEAD_WIDTH)
    scores = jnp.einsum(
        "bkgd,blkd->bkgl", heads_of_query, heads_of_key, preferred_element_type=jnp.float32
    ) * (1.0 / math.sqrt(HEAD_WIDTH))
    visible = (jnp.arange(length)[None, :] < filled_lengths[:, None])[:, None, None, :]
    scores = jnp.where(visible, scores, jnp.float32(-1e30))
    row_max = jnp.max(scores, axis=-1, keepdims=True)
    exp_scores = jnp.exp(scores - row_max)
    weights = (exp_scores / jnp.sum(exp_scores, axis=-1, keepdims=True)).astype(jnp.bfloat16)
    attended = jnp.einsum(
        "bkgl,blkd->bkgd", weights, heads_of_value, preferred_element_type=jnp.float32
    )
    return attended.astype(jnp.bfloat16).reshape(requests, row_width)


def attention_blocked(queries, key_cache_table, value_cache_table, filled_lengths):
    requests, row_width = queries.shape
    heads = row_width // HEAD_WIDTH
    length = key_cache_table.shape[1]
    block = BLOCK_REQUESTS
    count = requests // block
    stacked = (
        queries.reshape(count, block, heads, HEAD_WIDTH)
        .transpose(0, 2, 1, 3)
        .reshape(count, heads * block, HEAD_WIDTH)
    )
    keys = key_cache_table.reshape(count, block * length, HEAD_WIDTH)
    values = value_cache_table.reshape(count, block * length, HEAD_WIDTH)
    scores = jnp.einsum(
        "nrd,njd->nrj", stacked, keys, preferred_element_type=jnp.float32
    ) * (1.0 / math.sqrt(HEAD_WIDTH))
    row_request = jnp.arange(heads * block) % block
    col_request = jnp.arange(block * length) // length
    col_slot = jnp.arange(block * length) % length
    col_length = jnp.repeat(filled_lengths.reshape(count, block), length, axis=1)
    visible = (row_request[:, None] == col_request[None, :])[None] & (
        col_slot[None, None, :] < col_length[:, None, :]
    )
    scores = jnp.where(visible, scores, jnp.float32(-1e30))
    row_max = jnp.max(scores, axis=-1, keepdims=True)
    exp_scores = jnp.exp(scores - row_max)
    weights = (exp_scores / jnp.sum(exp_scores, axis=-1, keepdims=True)).astype(jnp.bfloat16)
    weights = lax.optimization_barrier(weights)
    attended = jnp.einsum("nrj,njd->nrd", weights, values, preferred_element_type=jnp.float32)
    return (
        attended.astype(jnp.bfloat16)
        .reshape(count, heads, block, HEAD_WIDTH)
        .transpose(0, 2, 1, 3)
        .reshape(requests, row_width)
    )


def prefix_count(mask):
    n = mask.shape[-1]
    earlier = (jnp.arange(n)[:, None] < jnp.arange(n)[None, :]).astype(jnp.bfloat16)
    return jnp.einsum(
        "...i,ij->...j", mask.astype(jnp.bfloat16), earlier, preferred_element_type=jnp.float32
    )


def body(
    queries,
    key_cache_table,
    value_cache_table,
    filled_lengths,
    request_adapter,
    adapter_store_row,
    adapter_factor,
    adapter_down_store,
    adapter_up_store,
):
    requests, row_width = queries.shape
    group_count = lax.axis_size("dp")
    group_index = lax.axis_index("dp")
    capacity = max(2, 2 * requests // group_count)
    slot_count = group_count * capacity
    stored_total, rank_width = adapter_down_store.shape[0], adapter_down_store.shape[1]
    adapter_count = adapter_store_row.shape[0]

    if key_cache_table.shape[2] == HEAD_WIDTH and requests % BLOCK_REQUESTS == 0:
        attended = attention_blocked(queries, key_cache_table, value_cache_table, filled_lengths)
    else:
        attended = attention(queries, key_cache_table, value_cache_table, filled_lengths)

    own_ids = jnp.take(request_adapter, group_index * requests + jnp.arange(requests), mode="clip")
    own_row = jnp.take(adapter_store_row, own_ids, mode="clip")
    own_dest = own_row // stored_total
    same_dest = own_dest[:, None] == own_dest[None, :]
    before = jnp.arange(requests)[:, None] > jnp.arange(requests)[None, :]
    own_order = jnp.sum((same_dest & before).astype(jnp.int32), axis=1)
    own_cell = own_dest * capacity + own_order
    cell_hot = lax.optimization_barrier(
        (own_cell[None, :] == jnp.arange(slot_count)[:, None]).astype(jnp.bfloat16)
    )
    outgoing = jnp.einsum(
        "cb,bf->cf", cell_hot, attended, preferred_element_type=jnp.float32
    ).astype(jnp.bfloat16)
    arrived = lax.all_to_all(
        outgoing.reshape(group_count, capacity, row_width), "dp", 0, 0, tiled=True
    ).reshape(slot_count, row_width)

    local_rows = group_index * stored_total + jnp.arange(stored_total)
    holds = adapter_store_row[None, :] == local_rows[:, None]
    local_ids = jnp.sum(jnp.where(holds, jnp.arange(adapter_count)[None, :], 0), axis=1)
    local_factor = jnp.sum(jnp.where(holds, adapter_factor[None, :], 0.0), axis=1)
    all_ids = request_adapter.reshape(group_count, requests)
    hit = (all_ids[:, :, None] == local_ids[None, None, :]).astype(jnp.bfloat16)
    mine = jnp.sum(hit, axis=2)
    order_in = prefix_count(mine)
    pick = (mine[:, None, :] > 0) & (
        order_in[:, None, :] == jnp.arange(capacity, dtype=jnp.float32)[None, :, None]
    )
    picked = jnp.einsum(
        "gcb,gbj->gcj", pick.astype(jnp.bfloat16), hit, preferred_element_type=jnp.float32
    ).reshape(slot_count, stored_total)
    item_scale = jnp.dot(picked, local_factor, precision=lax.Precision.HIGHEST)

    store_down = adapter_down_store.reshape(stored_total * rank_width, row_width)
    products = lax.dot_general(
        arrived, store_down, (((1,), (1,)), ((), ())), preferred_element_type=jnp.float32
    )
    partial_value = jnp.sum(
        products.reshape(slot_count, stored_total, rank_width) * picked[:, :, None], axis=1
    )
    summed = of_everyone(partial_value, "tensor")
    low_rank = (summed * item_scale[:, None]).astype(jnp.bfloat16)
    spread = (picked.astype(jnp.bfloat16)[:, :, None] * low_rank[:, None, :]).reshape(
        slot_count, stored_total * rank_width
    )
    store_up = adapter_up_store.reshape(stored_total * rank_width, row_width)
    result = jnp.dot(spread, store_up, preferred_element_type=jnp.float32).astype(jnp.bfloat16)
    returned = lax.all_to_all(
        result.reshape(group_count, capacity, row_width), "dp", 0, 0, tiled=True
    ).reshape(slot_count, row_width)
    adapter_delta = jnp.einsum(
        "cb,cf->bf", cell_hot, returned, preferred_element_type=jnp.float32
    ).astype(jnp.bfloat16)
    return (attended, adapter_delta)


def solution(mesh):
    placed = (
        P("dp", "tensor"),
        P("dp", None, "tensor"),
        P("dp", None, "tensor"),
        P("dp"),
        P(),
        P(),
        P(),
        P("dp", None, "tensor"),
        P("dp", None, "tensor"),
    )
    return jax.shard_map(
        body,
        mesh=mesh,
        in_specs=placed,
        out_specs=(P("dp", "tensor"), P("dp", "tensor")),
        check_vma=False,
    )
```

```python
import math

import jax
import jax.numpy as jnp
from jax import lax
from jax.sharding import PartitionSpec as P

HEAD_WIDTH = 128
BLOCK_REQUESTS = 4


def of_everyone(value, axis):
    copies = jnp.broadcast_to(value, (lax.axis_size(axis), *value.shape))
    return lax.all_to_all(copies, axis, split_axis=0, concat_axis=0, tiled=True).sum(axis=0)


def attention(queries, key_cache_table, value_cache_table, filled_lengths):
    requests, row_width = queries.shape
    kv_local = key_cache_table.shape[2] // HEAD_WIDTH
    group_width = row_width // HEAD_WIDTH // kv_local
    length = key_cache_table.shape[1]
    heads_of_query = queries.reshape(requests, kv_local, group_width, HEAD_WIDTH)
    heads_of_key = key_cache_table.reshape(requests, length, kv_local, HEAD_WIDTH)
    heads_of_value = value_cache_table.reshape(requests, length, kv_local, HEAD_WIDTH)
    scores = jnp.einsum(
        "bkgd,blkd->bkgl", heads_of_query, heads_of_key, preferred_element_type=jnp.float32
    ) * (1.0 / math.sqrt(HEAD_WIDTH))
    visible = (jnp.arange(length)[None, :] < filled_lengths[:, None])[:, None, None, :]
    scores = jnp.where(visible, scores, jnp.float32(-1e30))
    row_max = jnp.max(scores, axis=-1, keepdims=True)
    exp_scores = jnp.exp(scores - row_max)
    weights = (exp_scores / jnp.sum(exp_scores, axis=-1, keepdims=True)).astype(jnp.bfloat16)
    attended = jnp.einsum(
        "bkgl,blkd->bkgd", weights, heads_of_value, preferred_element_type=jnp.float32
    )
    return attended.astype(jnp.bfloat16).reshape(requests, row_width)


def attention_blocked(queries, key_cache_table, value_cache_table, filled_lengths):
    requests, row_width = queries.shape
    heads = row_width // HEAD_WIDTH
    length = key_cache_table.shape[1]
    block = BLOCK_REQUESTS
    count = requests // block
    stacked = (
        queries.reshape(count, block, heads, HEAD_WIDTH)
        .transpose(0, 2, 1, 3)
        .reshape(count, heads * block, HEAD_WIDTH)
    )
    keys = key_cache_table.reshape(count, block * length, HEAD_WIDTH)
    values = value_cache_table.reshape(count, block * length, HEAD_WIDTH)
    scores = jnp.einsum(
        "nrd,njd->nrj", stacked, keys, preferred_element_type=jnp.float32
    ) * (1.0 / math.sqrt(HEAD_WIDTH))
    row_request = jnp.arange(heads * block) % block
    col_request = jnp.arange(block * length) // length
    col_slot = jnp.arange(block * length) % length
    lengths = jnp.take(filled_lengths, jnp.arange(requests), mode="clip")
    col_length = jnp.repeat(lengths.reshape(count, block), length, axis=1)
    visible = (row_request[:, None] == col_request[None, :])[None] & (
        col_slot[None, None, :] < col_length[:, None, :]
    )
    scores = jnp.where(visible, scores, jnp.float32(-1e30))
    row_max = jnp.max(scores, axis=-1, keepdims=True)
    exp_scores = jnp.exp(scores - row_max)
    weights = (exp_scores / jnp.sum(exp_scores, axis=-1, keepdims=True)).astype(jnp.bfloat16)
    weights = lax.optimization_barrier(weights)
    attended = jnp.einsum("nrj,njd->nrd", weights, values, preferred_element_type=jnp.float32)
    return (
        attended.astype(jnp.bfloat16)
        .reshape(count, heads, block, HEAD_WIDTH)
        .transpose(0, 2, 1, 3)
        .reshape(requests, row_width)
    )


def prefix_count(mask):
    n = mask.shape[-1]
    earlier = (jnp.arange(n)[:, None] < jnp.arange(n)[None, :]).astype(jnp.bfloat16)
    return jnp.einsum(
        "...i,ij->...j", mask.astype(jnp.bfloat16), earlier, preferred_element_type=jnp.float32
    )


def body(
    queries,
    key_cache_table,
    value_cache_table,
    filled_lengths,
    request_adapter,
    adapter_store_row,
    adapter_factor,
    adapter_down_store,
    adapter_up_store,
):
    requests, row_width = queries.shape
    group_count = lax.axis_size("dp")
    group_index = lax.axis_index("dp")
    capacity = max(2, 2 * requests // group_count)
    slot_count = group_count * capacity
    stored_total, rank_width = adapter_down_store.shape[0], adapter_down_store.shape[1]
    adapter_count = adapter_store_row.shape[0]

    if key_cache_table.shape[2] == HEAD_WIDTH and requests % BLOCK_REQUESTS == 0:
        attended = attention_blocked(queries, key_cache_table, value_cache_table, filled_lengths)
    else:
        attended = attention(queries, key_cache_table, value_cache_table, filled_lengths)

    own_ids = lax.dynamic_slice_in_dim(request_adapter, group_index * requests, requests)
    own_row = jnp.take(adapter_store_row, own_ids, mode="clip")
    own_dest = own_row // stored_total
    same_dest = own_dest[:, None] == own_dest[None, :]
    before = jnp.arange(requests)[:, None] > jnp.arange(requests)[None, :]
    own_order = jnp.sum((same_dest & before).astype(jnp.int32), axis=1)
    own_cell = own_dest * capacity + own_order
    cell_hot = lax.optimization_barrier(
        (own_cell[None, :] == jnp.arange(slot_count)[:, None]).astype(jnp.bfloat16)
    )
    outgoing = jnp.einsum(
        "cb,bf->cf", cell_hot, attended, preferred_element_type=jnp.float32
    ).astype(jnp.bfloat16)
    arrived = lax.all_to_all(
        outgoing.reshape(group_count, capacity, row_width), "dp", 0, 0, tiled=True
    ).reshape(slot_count, row_width)

    local_rows = group_index * stored_total + jnp.arange(stored_total)
    holds = adapter_store_row[None, :] == local_rows[:, None]
    local_ids = jnp.sum(jnp.where(holds, jnp.arange(adapter_count)[None, :], 0), axis=1)
    local_factor = jnp.sum(jnp.where(holds, adapter_factor[None, :], 0.0), axis=1)
    all_ids = request_adapter.reshape(group_count, requests)
    hit = (all_ids[:, :, None] == local_ids[None, None, :]).astype(jnp.bfloat16)
    mine = jnp.sum(hit, axis=2)
    order_in = prefix_count(mine)
    pick = (mine[:, None, :] > 0) & (
        order_in[:, None, :] == jnp.arange(capacity, dtype=jnp.float32)[None, :, None]
    )
    picked = jnp.einsum(
        "gcb,gbj->gcj", pick.astype(jnp.bfloat16), hit, preferred_element_type=jnp.float32
    ).reshape(slot_count, stored_total)
    item_scale = jnp.dot(picked, local_factor, precision=lax.Precision.HIGHEST)

    store_down = adapter_down_store.reshape(stored_total * rank_width, row_width)
    products = lax.dot_general(
        arrived, store_down, (((1,), (1,)), ((), ())), preferred_element_type=jnp.float32
    )
    partial_value = jnp.sum(
        products.reshape(slot_count, stored_total, rank_width) * picked[:, :, None], axis=1
    )
    summed = of_everyone(partial_value, "tensor")
    low_rank = (summed * item_scale[:, None]).astype(jnp.bfloat16)
    spread = (picked.astype(jnp.bfloat16)[:, :, None] * low_rank[:, None, :]).reshape(
        slot_count, stored_total * rank_width
    )
    store_up = adapter_up_store.reshape(stored_total * rank_width, row_width)
    result = jnp.dot(spread, store_up, preferred_element_type=jnp.float32).astype(jnp.bfloat16)
    returned = lax.all_to_all(
        result.reshape(group_count, capacity, row_width), "dp", 0, 0, tiled=True
    ).reshape(slot_count, row_width)
    adapter_delta = jnp.einsum(
        "cb,cf->bf", cell_hot, returned, preferred_element_type=jnp.float32
    ).astype(jnp.bfloat16)
    return (attended, adapter_delta)


def solution(mesh):
    placed = (
        P("dp", "tensor"),
        P("dp", None, "tensor"),
        P("dp", None, "tensor"),
        P("dp"),
        P(),
        P(),
        P(),
        P("dp", None, "tensor"),
        P("dp", None, "tensor"),
    )
    return jax.shard_map(
        body,
        mesh=mesh,
        in_specs=placed,
        out_specs=(P("dp", "tensor"), P("dp", "tensor")),
        check_vma=False,
    )
```
